128 devices in a mesh: row: 16 (over y, x_lo, core), col: 8 (over z, x_hi).
Axes of the slice: x: 4 (x_hi: 2, x_lo: 2; x = x_hi * 2 + x_lo), y: 4, z: 4, core: 2. Of those that a mesh axis runs over, the one named last changes fastest.
Arguments:
- trailing: float32 [16384, 16384], P('row', 'col'), may hold values from -12 to 12, as said below
- panel: float32 [16384, 256], P('row'), may hold values from -3 to 3, as said below
Outputs:
- updated: float32 [16384, 16384], P('row', 'col')
- band_block: float32 [256, 256], replicated
The draws below stay inside these ranges and needn't reach their ends.
Inputs may be any that keep to these rules, and one draw needn't show every extreme that they name: trailing, read in global order, equals its transpose. Read in global order, the top 256 x 256 block of panel is 2 I plus entries of magnitude at most 6 / sqrt(16384), and the rows below have entries of magnitude at most 6 / sqrt(16384).
All inputs are finite; a program needn't handle non-finite values.
Results may differ from the reference program's by a relative error of at most 0.00011.
Values sent between devices are 32-bit elements; how exact they have to be, the bound alone decides.
No kernel may reach another device: no remote copies, remote signals or barrier semaphores. Data moves between devices by JAX's collectives and lax.ppermute only.
A program may use at most 128 MiB of HBM per device.

```python
import jax
import jax.numpy as jnp
from jax import lax

M = 16384
NB = 256
LOCAL_ROWS = 1024
LOCAL_COLS = 2048
N_ROW = 16
N_COL = 8


def store_rows_drawn(matrix, groups):
    blocks = matrix.shape[0] // (NB * groups)
    return matrix.reshape(blocks, groups, NB, -1).transpose(1, 0, 2, 3).reshape(matrix.shape[0], -1)


def draw_trailing(key, part):
    base = jax.random.normal(key, (M, M), jnp.float32)
    symmetric = (base + base.T) * 0.7071
    return store_rows_drawn(store_rows_drawn(symmetric, M // LOCAL_ROWS).T, M // LOCAL_COLS).T


def draw_panel(key, part):
    first_key = jax.random.fold_in(key, 11)
    noise = jax.random.normal(first_key, (M, NB), jnp.float32)
    noise = jnp.clip(noise, -6.0, 6.0) / M ** 0.5
    diagonal = jnp.concatenate([2.0 * jnp.eye(NB, dtype=jnp.float32), jnp.zeros((M - NB, NB), jnp.float32)], axis=0)
    return store_rows_drawn(noise + diagonal, M // LOCAL_ROWS)


def setup_inputs(seed: int = 0) -> dict:
    arg_keys = jax.random.split(jax.random.key(seed), 3)
    return {
        "trailing": draw_trailing(jax.random.fold_in(arg_keys[2], 71), 0),
        "panel": draw_panel(jax.random.fold_in(arg_keys[2], 71), 0),
    }


def matmul(left, right):
    return jnp.dot(left.astype(jnp.float32), right.astype(jnp.float32), precision=lax.Precision.HIGHEST, preferred_element_type=jnp.float32)

def lu_unpivoted(matrix):
    order_size = matrix.shape[0]
    positions = jnp.arange(order_size)

    def eliminate(column, factors):
        below = positions > column
        pivot_value = factors[column, column]
        multipliers = jnp.where(below, factors[:, column] / pivot_value, 0.0)
        pivot_row = jnp.where(below, factors[column, :], 0.0)
        factors = factors - multipliers[:, None] * pivot_row[None, :]
        return factors.at[:, column].set(jnp.where(below, multipliers, factors[:, column]))
    factors = lax.fori_loop(0, order_size, eliminate, matrix)
    unit_lower = jnp.tril(factors, -1) + jnp.eye(order_size, dtype=matrix.dtype)
    return (unit_lower, jnp.triu(factors))

def unstore_rows(matrix, groups):
    blocks = matrix.shape[0] // (NB * groups)
    return matrix.reshape(groups, blocks, NB, -1).transpose(1, 0, 2, 3).reshape(matrix.shape[0], -1)

def store_rows(matrix, groups):
    blocks = matrix.shape[0] // (NB * groups)
    return matrix.reshape(blocks, groups, NB, -1).transpose(1, 0, 2, 3).reshape(matrix.shape[0], -1)

def reference(trailing, panel):
    full = unstore_rows(unstore_rows(trailing, N_ROW).T, N_COL).T
    column_block = unstore_rows(panel, N_ROW)
    identity = jnp.eye(NB, dtype=jnp.float32)
    gram_total = matmul(column_block.T, column_block)
    lower_chol = jnp.linalg.cholesky(gram_total)
    ortho_rows = jax.scipy.linalg.solve_triangular(lower_chol, column_block.T, lower=True).T
    unit_lower, upper_tri = lu_unpivoted(identity + ortho_rows[:NB])
    shifted = ortho_rows.at[:NB].add(identity)
    reflectors = jax.scipy.linalg.solve_triangular(upper_tri, shifted.T, trans='T', lower=False).T
    tri_factor = jax.scipy.linalg.solve_triangular(unit_lower, upper_tri.T, lower=True, unit_diagonal=True).T
    product = matmul(full, reflectors)
    inner_gram = matmul(reflectors.T, product)
    middle = matmul(matmul(tri_factor.T, inner_gram), tri_factor)
    update_rows = matmul(product, tri_factor) - 0.5 * matmul(reflectors, middle)
    result = full - matmul(reflectors, update_rows.T) - matmul(update_rows, reflectors.T)
    stored = store_rows(store_rows(result, N_ROW).T, N_COL).T
    return (stored, -lower_chol.T)
```

```python
import jax
import jax.numpy as jnp
from jax import lax
from jax.experimental import pallas as pl
from jax.sharding import PartitionSpec as P

_INTERPRET = False
_CHUNK = 16


def matmul(left, right):
    return jnp.dot(left, right, precision=lax.Precision.HIGHEST, preferred_element_type=jnp.float32)


def matmul_tn(left, right):
    return lax.dot_general(
        left,
        right,
        (((0,), (0,)), ((), ())),
        precision=lax.Precision.HIGHEST,
        preferred_element_type=jnp.float32,
    )


def matmul_nt(left, right):
    return lax.dot_general(
        left,
        right,
        (((1,), (1,)), ((), ())),
        precision=lax.Precision.HIGHEST,
        preferred_element_type=jnp.float32,
    )


def _elim_kernel(m_ref, f_ref, r_ref):
    n = m_ref.shape[0]
    f_ref[...] = m_ref[...]
    ri = lax.broadcasted_iota(jnp.int32, (n, n), 0)
    ci = lax.broadcasted_iota(jnp.int32, (n, n), 1)
    r_ref[...] = jnp.where(ri == ci, 1.0, 0.0).astype(jnp.float32)
    for chunk in range(n // _CHUNK):
        r0 = chunk * _CHUNK
        c0 = (r0 // 128) * 128
        rc1 = min(n, ((r0 + _CHUNK - 1) // 128 + 1) * 128)
        nr = n - r0
        nc = n - c0

        def step(j, carry, r0=r0, c0=c0, rc1=rc1, nr=nr, nc=nc):
            f = f_ref[r0:, c0:]
            rows = lax.broadcasted_iota(jnp.int32, (nr, nc), 0) + r0
            row_j = jnp.sum(jnp.where(rows[:_CHUNK] == j, f[:_CHUNK], 0.0), axis=0, keepdims=True)
            lanes = lax.broadcasted_iota(jnp.int32, (nr, nc), 1) + c0
            lanes_row = lax.broadcasted_iota(jnp.int32, (1, nc), 1) + c0
            rows_col = lax.broadcasted_iota(jnp.int32, (nr, 1), 0) + r0
            col_j = jnp.sum(jnp.where(lanes == j, f, 0.0), axis=1, keepdims=True)
            pivot = jnp.sum(jnp.where(lanes_row == j, row_j, 0.0), axis=1, keepdims=True)
            mult = jnp.where(rows_col > j, col_j / pivot, 0.0)
            upd = jnp.where(lanes_row > j, row_j, 0.0)
            f = f - mult * upd
            f = jnp.where((lanes == j) & (rows > j), mult, f)
            f_ref[r0:, c0:] = f
            r_now = r_ref[r0:, :rc1]
            r_rows = lax.broadcasted_iota(jnp.int32, (_CHUNK, rc1), 0) + r0
            r_row = jnp.sum(jnp.where(r_rows == j, r_now[:_CHUNK], 0.0), axis=0, keepdims=True)
            r_ref[r0:, :rc1] = r_now - mult * r_row
            return carry

        lax.fori_loop(r0, r0 + _CHUNK, step, 0)


def eliminate(stack):
    count, n, _ = stack.shape
    spec = pl.BlockSpec((None, n, n), lambda b: (b, 0, 0))
    return pl.pallas_call(
        _elim_kernel,
        grid=(count,),
        in_specs=[spec],
        out_specs=[spec, spec],
        out_shape=[jax.ShapeDtypeStruct(stack.shape, jnp.float32)] * 2,
        interpret=_INTERPRET,
    )(stack)


def mirror(row_piece, col_count, col_index, band_size):
    group_ratio = lax.axis_size("row") // col_count
    blocks = row_piece.shape[0] // band_size
    gathered = lax.all_gather(row_piece, "row", axis=0, tiled=True)
    gathered = gathered.reshape(group_ratio, col_count, blocks, band_size, band_size)
    pieces = lax.dynamic_index_in_dim(gathered, col_index, 1, keepdims=False)
    return pieces.transpose(1, 0, 2, 3).reshape(group_ratio * row_piece.shape[0], band_size)


def small_factors(gram_total, top_rows):
    band_size = gram_total.shape[0]
    identity = jnp.eye(band_size, dtype=jnp.float32)
    gram_f, gram_r = eliminate(gram_total[None])
    gram_f = gram_f[0]
    scale = 1.0 / jnp.sqrt(jnp.diagonal(gram_f))
    chol_t = scale[:, None] * jnp.triu(gram_f)
    chol_inverse = scale[:, None] * gram_r[0]
    ortho_top = matmul_nt(top_rows, chol_inverse)
    shifted_top = identity + ortho_top
    lu_f, lu_r = eliminate(jnp.stack([shifted_top, shifted_top.T]))
    upper_tri = jnp.triu(lu_f[0])
    unit_inverse = lu_r[0]
    upper_inverse = lu_r[1].T / jnp.diagonal(lu_f[1])[None, :]
    tri_factor = matmul_nt(upper_tri, unit_inverse)
    right = matmul_tn(chol_inverse, upper_inverse)
    return chol_t, right, upper_inverse, tri_factor


def shards(trailing, panel):
    col_count = lax.axis_size("col")
    row_index = lax.axis_index("row")
    col_index = lax.axis_index("col")
    band_size = panel.shape[1]
    first_owner = (row_index == 0).astype(jnp.float32)
    gram_part = matmul_tn(panel, panel)
    top_part = panel[:band_size] * first_owner
    gram_total, top_rows = lax.psum((gram_part, top_part), "row")
    chol_t, right, upper_inverse, tri_factor = small_factors(gram_total, top_rows)
    reflectors = matmul(panel, right)
    reflectors = reflectors.at[:band_size].add(upper_inverse * first_owner)
    refl_cols = mirror(reflectors, col_count, col_index, band_size)
    product_rows = lax.psum(matmul(trailing, refl_cols), "col")
    inner_gram = lax.psum(matmul_tn(reflectors, product_rows), "row")
    middle = matmul(matmul(tri_factor.T, inner_gram), tri_factor)
    update_rows = matmul(product_rows, tri_factor) - 0.5 * matmul(reflectors, middle)
    update_cols = mirror(update_rows, col_count, col_index, band_size)
    updated = trailing - matmul_nt(reflectors, update_cols) - matmul_nt(update_rows, refl_cols)
    return (updated, -chol_t)


def solution(mesh):
    return jax.shard_map(
        shards,
        mesh=mesh,
        in_specs=(P("row", "col"), P("row", None)),
        out_specs=(P("row", "col"), P()),
        check_vma=False,
    )
```

```python
import jax
import jax.numpy as jnp
from jax import lax
from jax.experimental import pallas as pl
from jax.sharding import PartitionSpec as P

_INTERPRET = False
_CHUNK = 16


def matmul(left, right):
    return jnp.dot(left, right, precision=lax.Precision.HIGHEST, preferred_element_type=jnp.float32)


def matmul_tn(left, right):
    return lax.dot_general(
        left,
        right,
        (((0,), (0,)), ((), ())),
        precision=lax.Precision.HIGHEST,
        preferred_element_type=jnp.float32,
    )


def matmul_nt(left, right):
    return lax.dot_general(
        left,
        right,
        (((1,), (1,)), ((), ())),
        precision=lax.Precision.HIGHEST,
        preferred_element_type=jnp.float32,
    )


def _elim_kernel(m_ref, f_ref, r_ref):
    n = m_ref.shape[0]
    f_ref[...] = m_ref[...]
    ri = lax.broadcasted_iota(jnp.int32, (n, n), 0)
    ci = lax.broadcasted_iota(jnp.int32, (n, n), 1)
    r_ref[...] = jnp.where(ri == ci, 1.0, 0.0).astype(jnp.float32)
    for chunk in range(n // _CHUNK):
        r0 = chunk * _CHUNK
        c0 = (r0 // 128) * 128
        rc1 = min(n, ((r0 + _CHUNK - 1) // 128 + 1) * 128)
        nr = n - r0
        nc = n - c0

        def step(j, carry, r0=r0, c0=c0, rc1=rc1, nr=nr, nc=nc):
            f = f_ref[r0:, c0:]
            rows = lax.broadcasted_iota(jnp.int32, (nr, nc), 0) + r0
            row_j = jnp.sum(jnp.where(rows[:_CHUNK] == j, f[:_CHUNK], 0.0), axis=0, keepdims=True)
            lanes = lax.broadcasted_iota(jnp.int32, (nr, nc), 1) + c0
            lanes_row = lax.broadcasted_iota(jnp.int32, (1, nc), 1) + c0
            rows_col = lax.broadcasted_iota(jnp.int32, (nr, 1), 0) + r0
            col_j = jnp.sum(jnp.where(lanes == j, f, 0.0), axis=1, keepdims=True)
            pivot = jnp.sum(jnp.where(lanes_row == j, row_j, 0.0), axis=1, keepdims=True)
            mult = jnp.where(rows_col > j, col_j / pivot, 0.0)
            upd = jnp.where(lanes_row > j, row_j, 0.0)
            f = f - mult * upd
            f = jnp.where((lanes == j) & (rows > j), mult, f)
            f_ref[r0:, c0:] = f
            r_now = r_ref[r0:, :rc1]
            r_rows = lax.broadcasted_iota(jnp.int32, (_CHUNK, rc1), 0) + r0
            r_row = jnp.sum(jnp.where(r_rows == j, r_now[:_CHUNK], 0.0), axis=0, keepdims=True)
            r_ref[r0:, :rc1] = r_now - mult * r_row
            return carry

        lax.fori_loop(r0, r0 + _CHUNK, step, 0)


def eliminate(stack):
    count, n, _ = stack.shape
    spec = pl.BlockSpec((None, n, n), lambda b: (b, 0, 0))
    return pl.pallas_call(
        _elim_kernel,
        grid=(count,),
        in_specs=[spec],
        out_specs=[spec, spec],
        out_shape=[jax.ShapeDtypeStruct(stack.shape, jnp.float32)] * 2,
        interpret=_INTERPRET,
    )(stack)


def _xor_pairs(count, bit):
    return [(i, i ^ bit) for i in range(count)]


def psum_doubling(value, axis):
    count = lax.axis_size(axis)
    bit = 1
    while bit < count:
        value = value + lax.ppermute(value, axis, _xor_pairs(count, bit))
        bit *= 2
    return value


def mirror_tree(row_piece, band_size):
    row_count = lax.axis_size("row")
    col_count = lax.axis_size("col")
    assert row_count == 2 * col_count
    row_index = lax.axis_index("row")
    col_index = lax.axis_index("col")
    piece = row_piece
    bit = 1
    while bit < col_count:
        pairs = []
        receivers = []
        for c in range(col_count):
            for r in range(row_count):
                if ((r ^ c) & (col_count - 1)) & ~(bit - 1) == 0:
                    pairs.append((r * col_count + c, (r ^ bit) * col_count + c))
                    receivers.append((r ^ bit) * col_count + c)
        received = lax.ppermute(piece, ("row", "col"), pairs)
        me = row_index * col_count + col_index
        is_receiver = jnp.zeros((), jnp.bool_)
        for dev in receivers:
            is_receiver = is_receiver | (me == dev)
        piece = jnp.where(is_receiver, received, piece)
        bit *= 2
    other = lax.ppermute(piece, "row", _xor_pairs(row_count, col_count))
    high = row_index >= col_count
    first = jnp.where(high, other, piece)
    second = jnp.where(high, piece, other)
    blocks = row_piece.shape[0] // band_size
    stacked = jnp.stack([first, second]).reshape(2, blocks, band_size, row_piece.shape[1])
    return stacked.transpose(1, 0, 2, 3).reshape(2 * row_piece.shape[0], row_piece.shape[1])


def small_factors(gram_total, top_rows):
    band_size = gram_total.shape[0]
    identity = jnp.eye(band_size, dtype=jnp.float32)
    gram_f, gram_r = eliminate(gram_total[None])
    gram_f = gram_f[0]
    scale = 1.0 / jnp.sqrt(jnp.diagonal(gram_f))
    chol_t = scale[:, None] * jnp.triu(gram_f)
    chol_inverse = scale[:, None] * gram_r[0]
    ortho_top = matmul_nt(top_rows, chol_inverse)
    shifted_top = identity + ortho_top
    lu_f, lu_r = eliminate(jnp.stack([shifted_top, shifted_top.T]))
    upper_tri = jnp.triu(lu_f[0])
    unit_inverse = lu_r[0]
    upper_inverse = lu_r[1].T / jnp.diagonal(lu_f[1])[None, :]
    tri_factor = matmul_nt(upper_tri, unit_inverse)
    right = matmul_tn(chol_inverse, upper_inverse)
    return chol_t, right, upper_inverse, tri_factor


def shards(trailing, panel):
    row_index = lax.axis_index("row")
    col_index = lax.axis_index("col")
    band_size = panel.shape[1]
    first_owner = (row_index == 0).astype(jnp.float32)
    first_col = (col_index == 0).astype(jnp.float32)
    gram_part = matmul_tn(panel, panel)
    top_part = panel[:band_size] * first_owner
    stacked = psum_doubling(jnp.concatenate([gram_part, top_part]), "row")
    gram_total = stacked[:band_size]
    top_rows = stacked[band_size:]
    panel_late, gram_total = lax.optimization_barrier((panel, gram_total))
    panel_cols = mirror_tree(panel_late, band_size)
    chol_t, right, upper_inverse, tri_factor = small_factors(gram_total, top_rows)
    refl_rows = matmul(panel, right)
    refl_rows = refl_rows.at[:band_size].add(upper_inverse * first_owner)
    refl_cols = matmul(panel_cols, right)
    refl_cols = refl_cols.at[:band_size].add(upper_inverse * first_col)
    product_rows = psum_doubling(matmul(trailing, refl_cols), "col")
    inner_gram = psum_doubling(matmul_tn(refl_rows, product_rows), "row")
    product_cols = mirror_tree(product_rows, band_size)
    middle = matmul(matmul(tri_factor.T, inner_gram), tri_factor)
    update_rows = matmul(product_rows, tri_factor) - 0.5 * matmul(refl_rows, middle)
    update_cols = matmul(product_cols, tri_factor) - 0.5 * matmul(refl_cols, middle)
    updated = trailing - matmul_nt(refl_rows, update_cols) - matmul_nt(update_rows, refl_cols)
    return (updated, -chol_t)


def solution(mesh):
    return jax.shard_map(
        shards,
        mesh=mesh,
        in_specs=(P("row", "col"), P("row", None)),
        out_specs=(P("row", "col"), P()),
        check_vma=False,
    )
```

```python
import jax
import jax.numpy as jnp
from jax import lax
from jax.experimental import pallas as pl
from jax.sharding import PartitionSpec as P

_INTERPRET = False
_CHUNK = 16


def matmul(left, right):
    return jnp.dot(left, right, precision=lax.Precision.HIGHEST, preferred_element_type=jnp.float32)


def matmul_tn(left, right):
    return lax.dot_general(
        left,
        right,
        (((0,), (0,)), ((), ())),
        precision=lax.Precision.HIGHEST,
        preferred_element_type=jnp.float32,
    )


def matmul_nt(left, right):
    return lax.dot_general(
        left,
        right,
        (((1,), (1,)), ((), ())),
        precision=lax.Precision.HIGHEST,
        preferred_element_type=jnp.float32,
    )


def _elim_kernel(m_ref, f_ref, r_ref):
    count, n, _ = m_ref.shape
    f_ref[...] = m_ref[...]
    ri = lax.broadcasted_iota(jnp.int32, (n, n), 0)
    ci = lax.broadcasted_iota(jnp.int32, (n, n), 1)
    for b in range(count):
        r_ref[b] = jnp.where(ri == ci, 1.0, 0.0).astype(jnp.float32)
    for chunk in range(n // _CHUNK):
        r0 = chunk * _CHUNK
        c0 = (r0 // 128) * 128
        rc1 = min(n, ((r0 + _CHUNK - 1) // 128 + 1) * 128)
        nr = n - r0
        nc = n - c0

        def step(j, carry, r0=r0, c0=c0, rc1=rc1, nr=nr, nc=nc):
            rows = lax.broadcasted_iota(jnp.int32, (nr, nc), 0) + r0
            lanes = lax.broadcasted_iota(jnp.int32, (nr, nc), 1) + c0
            lanes_row = lax.broadcasted_iota(jnp.int32, (1, nc), 1) + c0
            rows_col = lax.broadcasted_iota(jnp.int32, (nr, 1), 0) + r0
            r_rows = lax.broadcasted_iota(jnp.int32, (_CHUNK, rc1), 0) + r0
            for b in range(count):
                f = f_ref[b, r0:, c0:]
                row_j = jnp.sum(jnp.where(rows[:_CHUNK] == j, f[:_CHUNK], 0.0), axis=0, keepdims=True)
                col_j = jnp.sum(jnp.where(lanes == j, f, 0.0), axis=1, keepdims=True)
                pivot = jnp.sum(jnp.where(lanes_row == j, row_j, 0.0), axis=1, keepdims=True)
                mult = jnp.where(rows_col > j, col_j / pivot, 0.0)
                upd = jnp.where(lanes_row > j, row_j, 0.0)
                f = f - mult * upd
                f = jnp.where((lanes == j) & (rows > j), mult, f)
                f_ref[b, r0:, c0:] = f
                r_now = r_ref[b, r0:, :rc1]
                r_row = jnp.sum(jnp.where(r_rows == j, r_now[:_CHUNK], 0.0), axis=0, keepdims=True)
                r_ref[b, r0:, :rc1] = r_now - mult * r_row
            return carry

        lax.fori_loop(r0, r0 + _CHUNK, step, 0)


def eliminate(stack):
    return pl.pallas_call(
        _elim_kernel,
        out_shape=[jax.ShapeDtypeStruct(stack.shape, jnp.float32)] * 2,
        interpret=_INTERPRET,
    )(stack)


def matmul_fast(left, right):
    return jnp.dot(left, right, precision=lax.Precision.HIGH, preferred_element_type=jnp.float32)


def matmul_nt_fast(left, right):
    return lax.dot_general(
        left,
        right,
        (((1,), (1,)), ((), ())),
        precision=lax.Precision.HIGH,
        preferred_element_type=jnp.float32,
    )


def _xor_pairs(count, bit):
    return [(i, i ^ bit) for i in range(count)]


def psum_doubling(value, axis):
    count = lax.axis_size(axis)
    bit = 1
    while bit < count:
        value = value + lax.ppermute(value, axis, _xor_pairs(count, bit))
        bit *= 2
    return value


def psum_halving(value, axis, bits):
    index = lax.axis_index(axis)
    count = lax.axis_size(axis)
    keep = value
    for bit in bits:
        half = keep.shape[0] // 2
        upper = (index & bit) != 0
        send = jnp.where(upper, keep[:half], keep[half:])
        mine = jnp.where(upper, keep[half:], keep[:half])
        keep = mine + lax.ppermute(send, axis, _xor_pairs(count, bit))
    for bit in reversed(bits):
        upper = (index & bit) != 0
        other = lax.ppermute(keep, axis, _xor_pairs(count, bit))
        keep = jnp.where(upper, jnp.concatenate([other, keep]), jnp.concatenate([keep, other]))
    return keep


def mirror_tree(row_piece, band_size):
    row_count = lax.axis_size("row")
    col_count = lax.axis_size("col")
    assert row_count == 2 * col_count
    row_index = lax.axis_index("row")
    col_index = lax.axis_index("col")
    piece = row_piece
    bit = 1
    while bit < col_count:
        pairs = []
        receivers = []
        for c in range(col_count):
            for r in range(row_count):
                if ((r ^ c) & (col_count - 1)) & ~(bit - 1) == 0:
                    pairs.append((r * col_count + c, (r ^ bit) * col_count + c))
                    receivers.append((r ^ bit) * col_count + c)
        received = lax.ppermute(piece, ("row", "col"), pairs)
        me = row_index * col_count + col_index
        is_receiver = jnp.zeros((), jnp.bool_)
        for dev in receivers:
            is_receiver = is_receiver | (me == dev)
        piece = jnp.where(is_receiver, received, piece)
        bit *= 2
    other = lax.ppermute(piece, "row", _xor_pairs(row_count, col_count))
    high = row_index >= col_count
    first = jnp.where(high, other, piece)
    second = jnp.where(high, piece, other)
    blocks = row_piece.shape[0] // band_size
    stacked = jnp.stack([first, second]).reshape(2, blocks, band_size, row_piece.shape[1])
    return stacked.transpose(1, 0, 2, 3).reshape(2 * row_piece.shape[0], row_piece.shape[1])


def small_factors(gram_total, top_rows):
    band_size = gram_total.shape[0]
    identity = jnp.eye(band_size, dtype=jnp.float32)
    gram_f, gram_r = eliminate(gram_total[None])
    gram_f = gram_f[0]
    scale = 1.0 / jnp.sqrt(jnp.diagonal(gram_f))
    chol_t = scale[:, None] * jnp.triu(gram_f)
    chol_inverse = scale[:, None] * gram_r[0]
    ortho_top = matmul_nt(top_rows, chol_inverse)
    shifted_top = identity + ortho_top
    lu_f, lu_r = eliminate(jnp.stack([shifted_top, shifted_top.T]))
    upper_tri = jnp.triu(lu_f[0])
    unit_inverse = lu_r[0]
    upper_inverse = lu_r[1].T / jnp.diagonal(lu_f[1])[None, :]
    tri_factor = matmul_nt(upper_tri, unit_inverse)
    right = matmul_tn(chol_inverse, upper_inverse)
    return chol_t, right, upper_inverse, tri_factor


def shards(trailing, panel):
    row_index = lax.axis_index("row")
    col_index = lax.axis_index("col")
    band_size = panel.shape[1]
    first_owner = (row_index == 0).astype(jnp.float32)
    first_col = (col_index == 0).astype(jnp.float32)
    gram_part = matmul_tn(panel, panel)
    top_part = panel[:band_size] * first_owner
    stacked = psum_doubling(jnp.concatenate([gram_part, top_part]), "row")
    gram_total = stacked[:band_size]
    top_rows = stacked[band_size:]
    panel_late, gram_total = lax.optimization_barrier((panel, gram_total))
    panel_cols = mirror_tree(panel_late, band_size)
    chol_t, right, upper_inverse, tri_factor = small_factors(gram_total, top_rows)
    refl_rows = matmul(panel, right)
    refl_rows = refl_rows.at[:band_size].add(upper_inverse * first_owner)
    refl_cols = matmul(panel_cols, right)
    refl_cols = refl_cols.at[:band_size].add(upper_inverse * first_col)
    product_rows = psum_halving(matmul_fast(trailing, refl_cols), "col", (2, 1, 4))
    inner_gram = psum_doubling(matmul_tn(refl_rows, product_rows), "row")
    product_cols = mirror_tree(product_rows, band_size)
    middle = matmul(matmul(tri_factor.T, inner_gram), tri_factor)
    update_rows = matmul(product_rows, tri_factor) - 0.5 * matmul(refl_rows, middle)
    update_cols = matmul(product_cols, tri_factor) - 0.5 * matmul(refl_cols, middle)
    updated = trailing - matmul_nt_fast(refl_rows, update_cols) - matmul_nt_fast(update_rows, refl_cols)
    return (updated, -chol_t)


def solution(mesh):
    return jax.shard_map(
        shards,
        mesh=mesh,
        in_specs=(P("row", "col"), P("row", None)),
        out_specs=(P("row", "col"), P()),
        check_vma=False,
    )
```

```python
import jax
import jax.numpy as jnp
from jax import lax
from jax.experimental import pallas as pl
from jax.sharding import PartitionSpec as P

_INTERPRET = False
_CHUNK = 16


def matmul(left, right):
    return jnp.dot(left, right, precision=lax.Precision.HIGHEST, preferred_element_type=jnp.float32)


def matmul_tn(left, right):
    return lax.dot_general(
        left,
        right,
        (((0,), (0,)), ((), ())),
        precision=lax.Precision.HIGHEST,
        preferred_element_type=jnp.float32,
    )


def matmul_nt(left, right):
    return lax.dot_general(
        left,
        right,
        (((1,), (1,)), ((), ())),
        precision=lax.Precision.HIGHEST,
        preferred_element_type=jnp.float32,
    )


def _elim_kernel(m_ref, f_ref, r_ref):
    count, n, _ = m_ref.shape
    f_ref[...] = m_ref[...]
    ri = lax.broadcasted_iota(jnp.int32, (n, n), 0)
    ci = lax.broadcasted_iota(jnp.int32, (n, n), 1)
    for b in range(count):
        r_ref[b] = jnp.where(ri == ci, 1.0, 0.0).astype(jnp.float32)
    for chunk in range(n // _CHUNK):
        r0 = chunk * _CHUNK
        c0 = (r0 // 128) * 128
        rc1 = min(n, ((r0 + _CHUNK - 1) // 128 + 1) * 128)
        nr = n - r0
        nc = n - c0

        def step(j, carry, r0=r0, c0=c0, rc1=rc1, nr=nr, nc=nc):
            rows = lax.broadcasted_iota(jnp.int32, (nr, nc), 0) + r0
            lanes = lax.broadcasted_iota(jnp.int32, (nr, nc), 1) + c0
            lanes_row = lax.broadcasted_iota(jnp.int32, (1, nc), 1) + c0
            rows_col = lax.broadcasted_iota(jnp.int32, (nr, 1), 0) + r0
            r_rows = lax.broadcasted_iota(jnp.int32, (_CHUNK, rc1), 0) + r0
            for b in range(count):
                f = f_ref[b, r0:, c0:]
                row_j = jnp.sum(jnp.where(rows[:_CHUNK] == j, f[:_CHUNK], 0.0), axis=0, keepdims=True)
                col_j = jnp.sum(jnp.where(lanes == j, f, 0.0), axis=1, keepdims=True)
                pivot = jnp.sum(jnp.where(lanes_row == j, row_j, 0.0), axis=1, keepdims=True)
                mult = jnp.where(rows_col > j, col_j / pivot, 0.0)
                upd = jnp.where(lanes_row > j, row_j, 0.0)
                f = f - mult * upd
                f = jnp.where((lanes == j) & (rows > j), mult, f)
                f_ref[b, r0:, c0:] = f
                r_now = r_ref[b, r0:, :rc1]
                r_row = jnp.sum(jnp.where(r_rows == j, r_now[:_CHUNK], 0.0), axis=0, keepdims=True)
                r_ref[b, r0:, :rc1] = r_now - mult * r_row
            return carry

        lax.fori_loop(r0, r0 + _CHUNK, step, 0)


def eliminate(stack):
    return pl.pallas_call(
        _elim_kernel,
        out_shape=[jax.ShapeDtypeStruct(stack.shape, jnp.float32)] * 2,
        interpret=_INTERPRET,
    )(stack)


def matmul_fast(left, right):
    return jnp.dot(left, right, precision=lax.Precision.HIGH, preferred_element_type=jnp.float32)


def matmul_tn_fast(left, right):
    return lax.dot_general(
        left,
        right,
        (((0,), (0,)), ((), ())),
        precision=lax.Precision.HIGH,
        preferred_element_type=jnp.float32,
    )


def matmul_nt_fast(left, right):
    return lax.dot_general(
        left,
        right,
        (((1,), (1,)), ((), ())),
        precision=lax.Precision.HIGH,
        preferred_element_type=jnp.float32,
    )


def _xor_pairs(count, bit):
    return [(i, i ^ bit) for i in range(count)]


def psum_doubling(value, axis):
    count = lax.axis_size(axis)
    bit = 1
    while bit < count:
        value = value + lax.ppermute(value, axis, _xor_pairs(count, bit))
        bit *= 2
    return value


def _rotations(bits, chunks):
    return [bits[i % len(bits):] + bits[:i % len(bits)] for i in range(chunks)]


def psum_doubling_rot(value, axis, bits, chunks):
    parts = jnp.split(value, chunks)
    count = lax.axis_size(axis)
    out = []
    for part, order in zip(parts, _rotations(bits, chunks)):
        for bit in order:
            part = part + lax.ppermute(part, axis, _xor_pairs(count, bit))
        out.append(part)
    return jnp.concatenate(out)


def _halving(keep, axis, bits, index, count):
    for bit in bits:
        half = keep.shape[0] // 2
        upper = (index & bit) != 0
        send = jnp.where(upper, keep[:half], keep[half:])
        mine = jnp.where(upper, keep[half:], keep[:half])
        keep = mine + lax.ppermute(send, axis, _xor_pairs(count, bit))
    for bit in reversed(bits):
        upper = (index & bit) != 0
        other = lax.ppermute(keep, axis, _xor_pairs(count, bit))
        keep = jnp.where(upper, jnp.concatenate([other, keep]), jnp.concatenate([keep, other]))
    return keep


def psum_halving(value, axis, bits, chunks):
    index = lax.axis_index(axis)
    count = lax.axis_size(axis)
    parts = jnp.split(value, chunks)
    out = [_halving(part, axis, order, index, count) for part, order in zip(parts, _rotations(bits, chunks))]
    return jnp.concatenate(out)


def mirror_tree(row_piece, band_size):
    row_count = lax.axis_size("row")
    col_count = lax.axis_size("col")
    assert row_count == 2 * col_count
    row_index = lax.axis_index("row")
    col_index = lax.axis_index("col")
    piece = row_piece
    bit = 1
    while bit < col_count:
        pairs = []
        receivers = []
        for c in range(col_count):
            for r in range(row_count):
                if ((r ^ c) & (col_count - 1)) & ~(bit - 1) == 0:
                    pairs.append((r * col_count + c, (r ^ bit) * col_count + c))
                    receivers.append((r ^ bit) * col_count + c)
        received = lax.ppermute(piece, ("row", "col"), pairs)
        me = row_index * col_count + col_index
        is_receiver = jnp.zeros((), jnp.bool_)
        for dev in receivers:
            is_receiver = is_receiver | (me == dev)
        piece = jnp.where(is_receiver, received, piece)
        bit *= 2
    other = lax.ppermute(piece, "row", _xor_pairs(row_count, col_count))
    high = row_index >= col_count
    first = jnp.where(high, other, piece)
    second = jnp.where(high, piece, other)
    blocks = row_piece.shape[0] // band_size
    stacked = jnp.stack([first, second]).reshape(2, blocks, band_size, row_piece.shape[1])
    return stacked.transpose(1, 0, 2, 3).reshape(2 * row_piece.shape[0], row_piece.shape[1])


def small_factors(gram_total, top_rows):
    band_size = gram_total.shape[0]
    identity = jnp.eye(band_size, dtype=jnp.float32)
    gram_f, gram_r = eliminate(gram_total[None])
    gram_f = gram_f[0]
    scale = 1.0 / jnp.sqrt(jnp.diagonal(gram_f))
    chol_t = scale[:, None] * jnp.triu(gram_f)
    chol_inverse = scale[:, None] * gram_r[0]
    ortho_top = matmul_nt(top_rows, chol_inverse)
    shifted_top = identity + ortho_top
    lu_f, lu_r = eliminate(jnp.stack([shifted_top, shifted_top.T]))
    upper_tri = jnp.triu(lu_f[0])
    unit_inverse = lu_r[0]
    upper_inverse = lu_r[1].T / jnp.diagonal(lu_f[1])[None, :]
    tri_factor = matmul_nt(upper_tri, unit_inverse)
    right = matmul_tn(chol_inverse, upper_inverse)
    return chol_t, right, upper_inverse, tri_factor


def shards(trailing, panel):
    row_index = lax.axis_index("row")
    col_index = lax.axis_index("col")
    band_size = panel.shape[1]
    row_bits = tuple(1 << i for i in range(lax.axis_size("row").bit_length() - 1))
    col_bits = tuple(1 << i for i in range(lax.axis_size("col").bit_length() - 1))
    first_owner = (row_index == 0).astype(jnp.float32)
    first_col = (col_index == 0).astype(jnp.float32)
    gram_part = matmul_tn(panel, panel)
    top_part = panel[:band_size] * first_owner
    stacked = psum_doubling_rot(jnp.concatenate([gram_part, top_part]), "row", row_bits, 4)
    gram_total = stacked[:band_size]
    top_rows = stacked[band_size:]
    panel_late, gram_total = lax.optimization_barrier((panel, gram_total))
    panel_cols = mirror_tree(panel_late, band_size)
    chol_t, right, upper_inverse, tri_factor = small_factors(gram_total, top_rows)
    refl_rows = matmul(panel, right)
    refl_rows = refl_rows.at[:band_size].add(upper_inverse * first_owner)
    refl_cols = matmul(panel_cols, right)
    refl_cols = refl_cols.at[:band_size].add(upper_inverse * first_col)
    product_rows = psum_halving(matmul_fast(trailing, refl_cols), "col", col_bits, 4)
    product_cols = psum_halving(matmul_tn_fast(trailing, refl_rows), "row", row_bits, 4)
    inner_gram = psum_doubling_rot(matmul_tn(refl_rows, product_rows), "row", row_bits, 4)
    update_rows = matmul(product_rows, tri_factor)
    partial = trailing - matmul_nt_fast(update_rows, refl_cols)
    update_cols = matmul(product_cols, tri_factor)
    middle = matmul(matmul(tri_factor.T, inner_gram), tri_factor)
    middle_sym = 0.5 * (middle + middle.T)
    left = jnp.concatenate([refl_rows, -matmul(refl_rows, middle_sym)], axis=1)
    right_cols = jnp.concatenate([update_cols, refl_cols], axis=1)
    updated = partial - matmul_nt_fast(left, right_cols)
    return (updated, -chol_t)


def solution(mesh):
    return jax.shard_map(
        shards,
        mesh=mesh,
        in_specs=(P("row", "col"), P("row", None)),
        out_specs=(P("row", "col"), P()),
        check_vma=False,
    )
```

```python
import jax
import jax.numpy as jnp
from jax import lax
from jax.experimental import pallas as pl
from jax.sharding import PartitionSpec as P

_INTERPRET = False
_CHUNK = 16


def matmul(left, right):
    return jnp.dot(left, right, precision=lax.Precision.HIGHEST, preferred_element_type=jnp.float32)


def matmul_tn(left, right):
    return lax.dot_general(
        left,
        right,
        (((0,), (0,)), ((), ())),
        precision=lax.Precision.HIGHEST,
        preferred_element_type=jnp.float32,
    )


def matmul_nt(left, right):
    return lax.dot_general(
        left,
        right,
        (((1,), (1,)), ((), ())),
        precision=lax.Precision.HIGHEST,
        preferred_element_type=jnp.float32,
    )


def _elim_kernel(m_ref, f_ref, r_ref):
    count, n, _ = m_ref.shape
    f_ref[...] = m_ref[...]
    ri = lax.broadcasted_iota(jnp.int32, (n, n), 0)
    ci = lax.broadcasted_iota(jnp.int32, (n, n), 1)
    for b in range(count):
        r_ref[b] = jnp.where(ri == ci, 1.0, 0.0).astype(jnp.float32)
    for chunk in range(n // _CHUNK):
        r0 = chunk * _CHUNK
        c0 = (r0 // 128) * 128
        rc1 = min(n, ((r0 + _CHUNK - 1) // 128 + 1) * 128)
        nr = n - r0
        nc = n - c0

        def step(j, carry, r0=r0, c0=c0, rc1=rc1, nr=nr, nc=nc):
            rows = lax.broadcasted_iota(jnp.int32, (nr, nc), 0) + r0
            lanes = lax.broadcasted_iota(jnp.int32, (nr, nc), 1) + c0
            lanes_row = lax.broadcasted_iota(jnp.int32, (1, nc), 1) + c0
            rows_col = lax.broadcasted_iota(jnp.int32, (nr, 1), 0) + r0
            r_rows = lax.broadcasted_iota(jnp.int32, (_CHUNK, rc1), 0) + r0
            for b in range(count):
                f = f_ref[b, r0:, c0:]
                row_j = jnp.sum(jnp.where(rows[:_CHUNK] == j, f[:_CHUNK], 0.0), axis=0, keepdims=True)
                col_j = jnp.sum(jnp.where(lanes == j, f, 0.0), axis=1, keepdims=True)
                pivot = jnp.sum(jnp.where(lanes_row == j, row_j, 0.0), axis=1, keepdims=True)
                mult = jnp.where(rows_col > j, col_j / pivot, 0.0)
                upd = jnp.where(lanes_row > j, row_j, 0.0)
                f = f - mult * upd
                f = jnp.where((lanes == j) & (rows > j), mult, f)
                f_ref[b, r0:, c0:] = f
                r_now = r_ref[b, r0:, :rc1]
                r_row = jnp.sum(jnp.where(r_rows == j, r_now[:_CHUNK], 0.0), axis=0, keepdims=True)
                r_ref[b, r0:, :rc1] = r_now - mult * r_row
            return carry

        lax.fori_loop(r0, r0 + _CHUNK, step, 0)


def eliminate(stack):
    return pl.pallas_call(
        _elim_kernel,
        out_shape=[jax.ShapeDtypeStruct(stack.shape, jnp.float32)] * 2,
        interpret=_INTERPRET,
    )(stack)


def matmul_fast(left, right):
    return jnp.dot(left, right, precision=lax.Precision.HIGH, preferred_element_type=jnp.float32)


def matmul_tn_fast(left, right):
    return lax.dot_general(
        left,
        right,
        (((0,), (0,)), ((), ())),
        precision=lax.Precision.HIGH,
        preferred_element_type=jnp.float32,
    )


def matmul_nt_fast(left, right):
    return lax.dot_general(
        left,
        right,
        (((1,), (1,)), ((), ())),
        precision=lax.Precision.HIGH,
        preferred_element_type=jnp.float32,
    )


def _xor_pairs(count, bit):
    return [(i, i ^ bit) for i in range(count)]


def psum_doubling(value, axis):
    count = lax.axis_size(axis)
    bit = 1
    while bit < count:
        value = value + lax.ppermute(value, axis, _xor_pairs(count, bit))
        bit *= 2
    return value


def _rotations(bits, chunks):
    return [bits[i % len(bits):] + bits[:i % len(bits)] for i in range(chunks)]


def psum_doubling_rot(value, axis, bits, chunks):
    parts = jnp.split(value, chunks)
    count = lax.axis_size(axis)
    out = []
    for part, order in zip(parts, _rotations(bits, chunks)):
        for bit in order:
            part = part + lax.ppermute(part, axis, _xor_pairs(count, bit))
        out.append(part)
    return jnp.concatenate(out)


def _halving(keep, axis, bits, index, count):
    for bit in bits:
        half = keep.shape[0] // 2
        upper = (index & bit) != 0
        send = jnp.where(upper, keep[:half], keep[half:])
        mine = jnp.where(upper, keep[half:], keep[:half])
        keep = mine + lax.ppermute(send, axis, _xor_pairs(count, bit))
    for bit in reversed(bits):
        upper = (index & bit) != 0
        other = lax.ppermute(keep, axis, _xor_pairs(count, bit))
        keep = jnp.where(upper, jnp.concatenate([other, keep]), jnp.concatenate([keep, other]))
    return keep


def psum_halving(value, axis, bits, chunks):
    index = lax.axis_index(axis)
    count = lax.axis_size(axis)
    parts = jnp.split(value, chunks)
    out = [_halving(part, axis, order, index, count) for part, order in zip(parts, _rotations(bits, chunks))]
    return jnp.concatenate(out)


def mirror_tree(row_piece, band_size):
    row_count = lax.axis_size("row")
    col_count = lax.axis_size("col")
    assert row_count == 2 * col_count
    row_index = lax.axis_index("row")
    col_index = lax.axis_index("col")
    piece = row_piece
    bit = 1
    while bit < col_count:
        pairs = []
        receivers = []
        for c in range(col_count):
            for r in range(row_count):
                if ((r ^ c) & (col_count - 1)) & ~(bit - 1) == 0:
                    pairs.append((r * col_count + c, (r ^ bit) * col_count + c))
                    receivers.append((r ^ bit) * col_count + c)
        received = lax.ppermute(piece, ("row", "col"), pairs)
        me = row_index * col_count + col_index
        is_receiver = jnp.zeros((), jnp.bool_)
        for dev in receivers:
            is_receiver = is_receiver | (me == dev)
        piece = jnp.where(is_receiver, received, piece)
        bit *= 2
    other = lax.ppermute(piece, "row", _xor_pairs(row_count, col_count))
    high = row_index >= col_count
    first = jnp.where(high, other, piece)
    second = jnp.where(high, piece, other)
    blocks = row_piece.shape[0] // band_size
    stacked = jnp.stack([first, second]).reshape(2, blocks, band_size, row_piece.shape[1])
    return stacked.transpose(1, 0, 2, 3).reshape(2 * row_piece.shape[0], row_piece.shape[1])


def small_factors(gram_total, top_rows):
    band_size = gram_total.shape[0]
    identity = jnp.eye(band_size, dtype=jnp.float32)
    gram_f, gram_r = eliminate(gram_total[None])
    gram_f = gram_f[0]
    scale = 1.0 / jnp.sqrt(jnp.diagonal(gram_f))
    chol_t = scale[:, None] * jnp.triu(gram_f)
    chol_inverse = scale[:, None] * gram_r[0]
    ortho_top = matmul_nt(top_rows, chol_inverse)
    shifted_top = identity + ortho_top
    lu_f, lu_r = eliminate(jnp.stack([shifted_top, shifted_top.T]))
    upper_tri = jnp.triu(lu_f[0])
    unit_inverse = lu_r[0]
    upper_inverse = lu_r[1].T / jnp.diagonal(lu_f[1])[None, :]
    tri_factor = matmul_nt(upper_tri, unit_inverse)
    right = matmul_tn(chol_inverse, upper_inverse)
    return chol_t, right, upper_inverse, tri_factor


def shards(trailing, panel):
    row_index = lax.axis_index("row")
    col_index = lax.axis_index("col")
    band_size = panel.shape[1]
    row_bits = tuple(1 << i for i in range(lax.axis_size("row").bit_length() - 1))
    col_bits = tuple(1 << i for i in range(lax.axis_size("col").bit_length() - 1))
    first_owner = (row_index == 0).astype(jnp.float32)
    first_col = (col_index == 0).astype(jnp.float32)
    gram_part = matmul_tn(panel, panel)
    top_part = panel[:band_size] * first_owner
    panel_cols = mirror_tree(panel, band_size)
    stacked = psum_doubling_rot(jnp.concatenate([gram_part, top_part]), "row", row_bits[::-1], 1)
    gram_total = stacked[:band_size]
    top_rows = stacked[band_size:]
    chol_t, right, upper_inverse, tri_factor = small_factors(gram_total, top_rows)
    refl_rows = matmul(panel, right)
    refl_rows = refl_rows.at[:band_size].add(upper_inverse * first_owner)
    refl_cols = matmul(panel_cols, right)
    refl_cols = refl_cols.at[:band_size].add(upper_inverse * first_col)
    product_rows = psum_halving(matmul_fast(trailing, refl_cols), "col", col_bits, 1)
    product_cols = psum_halving(matmul_tn_fast(trailing, refl_rows), "row", row_bits, 1)
    inner_gram = psum_doubling_rot(matmul_tn(refl_rows, product_rows), "row", row_bits, 1)
    update_rows = matmul(product_rows, tri_factor)
    partial = trailing - matmul_nt_fast(update_rows, refl_cols)
    update_cols = matmul(product_cols, tri_factor)
    middle = matmul(matmul(tri_factor.T, inner_gram), tri_factor)
    middle_sym = 0.5 * (middle + middle.T)
    left = jnp.concatenate([refl_rows, -matmul(refl_rows, middle_sym)], axis=1)
    right_cols = jnp.concatenate([update_cols, refl_cols], axis=1)
    updated = partial - matmul_nt_fast(left, right_cols)
    return (updated, -chol_t)


def solution(mesh):
    return jax.shard_map(
        shards,
        mesh=mesh,
        in_specs=(P("row", "col"), P("row", None)),
        out_specs=(P("row", "col"), P()),
        check_vma=False,
    )
```

```python
import jax
import jax.numpy as jnp
from jax import lax
from jax.experimental import pallas as pl
from jax.sharding import PartitionSpec as P

_INTERPRET = False
_CHUNK = 16


def matmul(left, right):
    return jnp.dot(left, right, precision=lax.Precision.HIGHEST, preferred_element_type=jnp.float32)


def matmul_tn(left, right):
    return lax.dot_general(
        left,
        right,
        (((0,), (0,)), ((), ())),
        precision=lax.Precision.HIGHEST,
        preferred_element_type=jnp.float32,
    )


def matmul_nt(left, right):
    return lax.dot_general(
        left,
        right,
        (((1,), (1,)), ((), ())),
        precision=lax.Precision.HIGHEST,
        preferred_element_type=jnp.float32,
    )


def _elim_kernel(m_ref, f_ref, r_ref):
    count, n, _ = m_ref.shape
    f_ref[...] = m_ref[...]
    ri = lax.broadcasted_iota(jnp.int32, (n, n), 0)
    ci = lax.broadcasted_iota(jnp.int32, (n, n), 1)
    for b in range(count):
        r_ref[b] = jnp.where(ri == ci, 1.0, 0.0).astype(jnp.float32)
    for chunk in range(n // _CHUNK):
        r0 = chunk * _CHUNK
        c0 = (r0 // 128) * 128
        rc1 = min(n, ((r0 + _CHUNK - 1) // 128 + 1) * 128)
        nr = n - r0
        nc = n - c0

        def step(j, carry, r0=r0, c0=c0, rc1=rc1, nr=nr, nc=nc):
            rows = lax.broadcasted_iota(jnp.int32, (nr, nc), 0) + r0
            lanes = lax.broadcasted_iota(jnp.int32, (nr, nc), 1) + c0
            lanes_row = lax.broadcasted_iota(jnp.int32, (1, nc), 1) + c0
            rows_col = lax.broadcasted_iota(jnp.int32, (nr, 1), 0) + r0
            r_rows = lax.broadcasted_iota(jnp.int32, (_CHUNK, rc1), 0) + r0
            for b in range(count):
                f = f_ref[b, r0:, c0:]
                row_j = jnp.sum(jnp.where(rows[:_CHUNK] == j, f[:_CHUNK], 0.0), axis=0, keepdims=True)
                col_j = jnp.sum(jnp.where(lanes == j, f, 0.0), axis=1, keepdims=True)
                pivot = jnp.sum(jnp.where(lanes_row == j, row_j, 0.0), axis=1, keepdims=True)
                mult = jnp.where(rows_col > j, col_j / pivot, 0.0)
                upd = jnp.where(lanes_row > j, row_j, 0.0)
                f = f - mult * upd
                f = jnp.where((lanes == j) & (rows > j), mult, f)
                f_ref[b, r0:, c0:] = f
                r_now = r_ref[b, r0:, :rc1]
                r_row = jnp.sum(jnp.where(r_rows == j, r_now[:_CHUNK], 0.0), axis=0, keepdims=True)
                r_ref[b, r0:, :rc1] = r_now - mult * r_row
            return carry

        lax.fori_loop(r0, r0 + _CHUNK, step, 0)


def eliminate(stack):
    return pl.pallas_call(
        _elim_kernel,
        out_shape=[jax.ShapeDtypeStruct(stack.shape, jnp.float32)] * 2,
        interpret=_INTERPRET,
    )(stack)


def matmul_fast(left, right):
    return jnp.dot(left, right, precision=lax.Precision.HIGH, preferred_element_type=jnp.float32)


def matmul_tn_fast(left, right):
    return lax.dot_general(
        left,
        right,
        (((0,), (0,)), ((), ())),
        precision=lax.Precision.HIGH,
        preferred_element_type=jnp.float32,
    )


def matmul_nt_fast(left, right):
    return lax.dot_general(
        left,
        right,
        (((1,), (1,)), ((), ())),
        precision=lax.Precision.HIGH,
        preferred_element_type=jnp.float32,
    )


def _xor_pairs(count, bit):
    return [(i, i ^ bit) for i in range(count)]


def psum_doubling(value, axis):
    count = lax.axis_size(axis)
    bit = 1
    while bit < count:
        value = value + lax.ppermute(value, axis, _xor_pairs(count, bit))
        bit *= 2
    return value


def _rotations(bits, chunks):
    return [bits[i % len(bits):] + bits[:i % len(bits)] for i in range(chunks)]


def psum_doubling_rot(value, axis, bits, chunks):
    parts = jnp.split(value, chunks)
    count = lax.axis_size(axis)
    out = []
    for part, order in zip(parts, _rotations(bits, chunks)):
        for bit in order:
            part = part + lax.ppermute(part, axis, _xor_pairs(count, bit))
        out.append(part)
    return jnp.concatenate(out)


def _halving(keep, axis, bits, index, count):
    for bit in bits:
        half = keep.shape[0] // 2
        upper = (index & bit) != 0
        send = jnp.where(upper, keep[:half], keep[half:])
        mine = jnp.where(upper, keep[half:], keep[:half])
        keep = mine + lax.ppermute(send, axis, _xor_pairs(count, bit))
    for bit in reversed(bits):
        upper = (index & bit) != 0
        other = lax.ppermute(keep, axis, _xor_pairs(count, bit))
        keep = jnp.where(upper, jnp.concatenate([other, keep]), jnp.concatenate([keep, other]))
    return keep


def psum_halving(value, axis, bits, chunks):
    index = lax.axis_index(axis)
    count = lax.axis_size(axis)
    parts = jnp.split(value, chunks)
    out = [_halving(part, axis, order, index, count) for part, order in zip(parts, _rotations(bits, chunks))]
    return jnp.concatenate(out)


def mirror_tree(row_piece, band_size):
    row_count = lax.axis_size("row")
    col_count = lax.axis_size("col")
    assert row_count == 2 * col_count
    row_index = lax.axis_index("row")
    col_index = lax.axis_index("col")
    piece = row_piece
    bit = 1
    while bit < col_count:
        pairs = []
        receivers = []
        for c in range(col_count):
            for r in range(row_count):
                if ((r ^ c) & (col_count - 1)) & ~(bit - 1) == 0:
                    pairs.append((r * col_count + c, (r ^ bit) * col_count + c))
                    receivers.append((r ^ bit) * col_count + c)
        received = lax.ppermute(piece, ("row", "col"), pairs)
        me = row_index * col_count + col_index
        is_receiver = jnp.zeros((), jnp.bool_)
        for dev in receivers:
            is_receiver = is_receiver | (me == dev)
        piece = jnp.where(is_receiver, received, piece)
        bit *= 2
    other = lax.ppermute(piece, "row", _xor_pairs(row_count, col_count))
    high = row_index >= col_count
    first = jnp.where(high, other, piece)
    second = jnp.where(high, piece, other)
    blocks = row_piece.shape[0] // band_size
    stacked = jnp.stack([first, second]).reshape(2, blocks, band_size, row_piece.shape[1])
    return stacked.transpose(1, 0, 2, 3).reshape(2 * row_piece.shape[0], row_piece.shape[1])


def small_factors(gram_total, top_rows):
    band_size = gram_total.shape[0]
    identity = jnp.eye(band_size, dtype=jnp.float32)
    gram_f, gram_r = eliminate(gram_total[None])
    gram_f = gram_f[0]
    scale = 1.0 / jnp.sqrt(jnp.diagonal(gram_f))
    chol_t = scale[:, None] * jnp.triu(gram_f)
    chol_inverse = scale[:, None] * gram_r[0]
    ortho_top = matmul_nt(top_rows, chol_inverse)
    shifted_top = identity + ortho_top
    lu_f, lu_r = eliminate(jnp.stack([shifted_top, shifted_top.T]))
    upper_tri = jnp.triu(lu_f[0])
    unit_inverse = lu_r[0]
    upper_inverse = lu_r[1].T / jnp.diagonal(lu_f[1])[None, :]
    tri_factor = matmul_nt(upper_tri, unit_inverse)
    right = matmul_tn(chol_inverse, upper_inverse)
    return chol_t, right, upper_inverse, tri_factor


def shards(trailing, panel):
    row_index = lax.axis_index("row")
    col_index = lax.axis_index("col")
    band_size = panel.shape[1]
    row_bits = tuple(1 << i for i in range(lax.axis_size("row").bit_length() - 1))
    col_bits = tuple(1 << i for i in range(lax.axis_size("col").bit_length() - 1))
    first_owner = (row_index == 0).astype(jnp.float32)
    first_col = (col_index == 0).astype(jnp.float32)
    gram_part = matmul_tn(panel, panel)
    top_part = panel[:band_size] * first_owner
    panel_cols = mirror_tree(panel, band_size)
    stacked = psum_halving(jnp.concatenate([gram_part, top_part]), "row", row_bits, 1)
    gram_total = stacked[:band_size]
    top_rows = stacked[band_size:]
    chol_t, right, upper_inverse, tri_factor = small_factors(gram_total, top_rows)
    refl_rows = matmul(panel, right)
    refl_rows = refl_rows.at[:band_size].add(upper_inverse * first_owner)
    refl_cols = matmul(panel_cols, right)
    refl_cols = refl_cols.at[:band_size].add(upper_inverse * first_col)
    product_rows = psum_halving(matmul_fast(trailing, refl_cols), "col", col_bits, 1)
    product_cols = psum_halving(matmul_tn_fast(trailing, refl_rows), "row", row_bits, 1)
    update_rows = matmul(product_rows, tri_factor)
    partial = trailing - matmul_nt_fast(update_rows, refl_cols)
    inner_part, partial = lax.optimization_barrier((matmul_tn(refl_rows, product_rows), partial))
    inner_gram = psum_doubling_rot(inner_part, "row", row_bits, 1)
    update_cols = matmul(product_cols, tri_factor)
    middle = matmul(matmul(tri_factor.T, inner_gram), tri_factor)
    middle_sym = 0.5 * (middle + middle.T)
    left = jnp.concatenate([refl_rows, -matmul(refl_rows, middle_sym)], axis=1)
    right_cols = jnp.concatenate([update_cols, refl_cols], axis=1)
    updated = partial - matmul_nt_fast(left, right_cols)
    return (updated, -chol_t)


def solution(mesh):
    return jax.shard_map(
        shards,
        mesh=mesh,
        in_specs=(P("row", "col"), P("row", None)),
        out_specs=(P("row", "col"), P()),
        check_vma=False,
    )
```

```python
import jax
import jax.numpy as jnp
from jax import lax
from jax.experimental import pallas as pl
from jax.sharding import PartitionSpec as P

_INTERPRET = False
_CHUNK = 16


def matmul(left, right):
    return jnp.dot(left, right, precision=lax.Precision.HIGHEST, preferred_element_type=jnp.float32)


def matmul_tn(left, right):
    return lax.dot_general(
        left,
        right,
        (((0,), (0,)), ((), ())),
        precision=lax.Precision.HIGHEST,
        preferred_element_type=jnp.float32,
    )


def matmul_nt(left, right):
    return lax.dot_general(
        left,
        right,
        (((1,), (1,)), ((), ())),
        precision=lax.Precision.HIGHEST,
        preferred_element_type=jnp.float32,
    )


def _elim_kernel(m_ref, f_ref, r_ref):
    count, n, _ = m_ref.shape
    f_ref[...] = m_ref[...]
    ri = lax.broadcasted_iota(jnp.int32, (n, n), 0)
    ci = lax.broadcasted_iota(jnp.int32, (n, n), 1)
    for b in range(count):
        r_ref[b] = jnp.where(ri == ci, 1.0, 0.0).astype(jnp.float32)
    for chunk in range(n // _CHUNK):
        r0 = chunk * _CHUNK
        c0 = (r0 // 128) * 128
        rc1 = min(n, ((r0 + _CHUNK - 1) // 128 + 1) * 128)
        nr = n - r0
        nc = n - c0

        def step(j, carry, r0=r0, c0=c0, rc1=rc1, nr=nr, nc=nc):
            rows = lax.broadcasted_iota(jnp.int32, (nr, nc), 0) + r0
            lanes = lax.broadcasted_iota(jnp.int32, (nr, nc), 1) + c0
            lanes_row = lax.broadcasted_iota(jnp.int32, (1, nc), 1) + c0
            rows_col = lax.broadcasted_iota(jnp.int32, (nr, 1), 0) + r0
            r_rows = lax.broadcasted_iota(jnp.int32, (_CHUNK, rc1), 0) + r0
            for b in range(count):
                f = f_ref[b, r0:, c0:]
                row_j = jnp.sum(jnp.where(rows[:_CHUNK] == j, f[:_CHUNK], 0.0), axis=0, keepdims=True)
                col_j = jnp.sum(jnp.where(lanes == j, f, 0.0), axis=1, keepdims=True)
                pivot = jnp.sum(jnp.where(lanes_row == j, row_j, 0.0), axis=1, keepdims=True)
                mult = jnp.where(rows_col > j, col_j / pivot, 0.0)
                upd = jnp.where(lanes_row > j, row_j, 0.0)
                f = f - mult * upd
                f = jnp.where((lanes == j) & (rows > j), mult, f)
                f_ref[b, r0:, c0:] = f
                r_now = r_ref[b, r0:, :rc1]
                r_row = jnp.sum(jnp.where(r_rows == j, r_now[:_CHUNK], 0.0), axis=0, keepdims=True)
                r_ref[b, r0:, :rc1] = r_now - mult * r_row
            return carry

        lax.fori_loop(r0, r0 + _CHUNK, step, 0)


def eliminate(stack):
    return pl.pallas_call(
        _elim_kernel,
        out_shape=[jax.ShapeDtypeStruct(stack.shape, jnp.float32)] * 2,
        interpret=_INTERPRET,
    )(stack)


def matmul_fast(left, right):
    return jnp.dot(left, right, precision=lax.Precision.HIGH, preferred_element_type=jnp.float32)


def matmul_tn_fast(left, right):
    return lax.dot_general(
        left,
        right,
        (((0,), (0,)), ((), ())),
        precision=lax.Precision.HIGH,
        preferred_element_type=jnp.float32,
    )


def matmul_nt_fast(left, right):
    return lax.dot_general(
        left,
        right,
        (((1,), (1,)), ((), ())),
        precision=lax.Precision.HIGH,
        preferred_element_type=jnp.float32,
    )


def _xor_pairs(count, bit):
    return [(i, i ^ bit) for i in range(count)]


def psum_doubling(value, axis):
    count = lax.axis_size(axis)
    bit = 1
    while bit < count:
        value = value + lax.ppermute(value, axis, _xor_pairs(count, bit))
        bit *= 2
    return value


def _rotations(bits, chunks):
    return [bits[i % len(bits):] + bits[:i % len(bits)] for i in range(chunks)]


def psum_doubling_rot(value, axis, bits, chunks):
    parts = jnp.split(value, chunks)
    count = lax.axis_size(axis)
    out = []
    for part, order in zip(parts, _rotations(bits, chunks)):
        for bit in order:
            part = part + lax.ppermute(part, axis, _xor_pairs(count, bit))
        out.append(part)
    return jnp.concatenate(out)


def _halving(keep, axis, bits, index, count, tie=None):
    for bit in bits:
        half = keep.shape[0] // 2
        upper = (index & bit) != 0
        send = jnp.where(upper, keep[:half], keep[half:])
        mine = jnp.where(upper, keep[half:], keep[:half])
        keep = mine + lax.ppermute(send, axis, _xor_pairs(count, bit))
    for bit in reversed(bits):
        if bit == bits[0] and tie is not None:
            keep, tie = lax.optimization_barrier((keep, tie))
        upper = (index & bit) != 0
        other = lax.ppermute(keep, axis, _xor_pairs(count, bit))
        keep = jnp.where(upper, jnp.concatenate([other, keep]), jnp.concatenate([keep, other]))
    if tie is not None:
        return keep, tie
    return keep


def psum_halving(value, axis, bits, chunks):
    index = lax.axis_index(axis)
    count = lax.axis_size(axis)
    parts = jnp.split(value, chunks)
    out = [_halving(part, axis, order, index, count) for part, order in zip(parts, _rotations(bits, chunks))]
    return jnp.concatenate(out)


def mirror_tree(row_piece, band_size):
    row_count = lax.axis_size("row")
    col_count = lax.axis_size("col")
    assert row_count == 2 * col_count
    row_index = lax.axis_index("row")
    col_index = lax.axis_index("col")
    piece = row_piece
    bit = 1
    while bit < col_count:
        pairs = []
        receivers = []
        for c in range(col_count):
            for r in range(row_count):
                if ((r ^ c) & (col_count - 1)) & ~(bit - 1) == 0:
                    pairs.append((r * col_count + c, (r ^ bit) * col_count + c))
                    receivers.append((r ^ bit) * col_count + c)
        received = lax.ppermute(piece, ("row", "col"), pairs)
        me = row_index * col_count + col_index
        is_receiver = jnp.zeros((), jnp.bool_)
        for dev in receivers:
            is_receiver = is_receiver | (me == dev)
        piece = jnp.where(is_receiver, received, piece)
        bit *= 2
    other = lax.ppermute(piece, "row", _xor_pairs(row_count, col_count))
    high = row_index >= col_count
    first = jnp.where(high, other, piece)
    second = jnp.where(high, piece, other)
    blocks = row_piece.shape[0] // band_size
    stacked = jnp.stack([first, second]).reshape(2, blocks, band_size, row_piece.shape[1])
    return stacked.transpose(1, 0, 2, 3).reshape(2 * row_piece.shape[0], row_piece.shape[1])


def small_factors(gram_total, top_rows):
    band_size = gram_total.shape[0]
    identity = jnp.eye(band_size, dtype=jnp.float32)
    gram_f, gram_r = eliminate(gram_total[None])
    gram_f = gram_f[0]
    scale = 1.0 / jnp.sqrt(jnp.diagonal(gram_f))
    chol_t = scale[:, None] * jnp.triu(gram_f)
    chol_inverse = scale[:, None] * gram_r[0]
    ortho_top = matmul_nt(top_rows, chol_inverse)
    shifted_top = identity + ortho_top
    lu_f, lu_r = eliminate(jnp.stack([shifted_top, shifted_top.T]))
    upper_tri = jnp.triu(lu_f[0])
    unit_inverse = lu_r[0]
    upper_inverse = lu_r[1].T / jnp.diagonal(lu_f[1])[None, :]
    tri_factor = matmul_nt(upper_tri, unit_inverse)
    right = matmul_tn(chol_inverse, upper_inverse)
    return chol_t, right, upper_inverse, tri_factor


def shards(trailing, panel):
    row_index = lax.axis_index("row")
    col_index = lax.axis_index("col")
    band_size = panel.shape[1]
    row_bits = tuple(1 << i for i in range(lax.axis_size("row").bit_length() - 1))
    col_bits = tuple(1 << i for i in range(lax.axis_size("col").bit_length() - 1))
    first_owner = (row_index == 0).astype(jnp.float32)
    first_col = (col_index == 0).astype(jnp.float32)
    gram_part = matmul_tn(panel, panel)
    top_part = panel[:band_size] * first_owner
    panel_cols = mirror_tree(panel, band_size)
    stacked = psum_halving(jnp.concatenate([gram_part, top_part]), "row", row_bits, 1)
    gram_total = stacked[:band_size]
    top_rows = stacked[band_size:]
    chol_t, right, upper_inverse, tri_factor = small_factors(gram_total, top_rows)
    refl_rows = matmul(panel, right)
    refl_rows = refl_rows.at[:band_size].add(upper_inverse * first_owner)
    refl_cols = matmul(panel_cols, right)
    refl_cols = refl_cols.at[:band_size].add(upper_inverse * first_col)
    product_rows = psum_halving(matmul_fast(trailing, refl_cols), "col", col_bits, 1)
    inner_gram = psum_doubling_rot(matmul_tn(refl_rows, product_rows), "row", row_bits, 1)
    update_rows = matmul(product_rows, tri_factor)
    partial = trailing - matmul_nt_fast(update_rows, refl_cols)
    index = lax.axis_index("row")
    count = lax.axis_size("row")
    product_cols, partial = _halving(matmul_tn_fast(trailing, refl_rows), "row", row_bits, index, count, partial)
    update_cols = matmul(product_cols, tri_factor)
    middle = matmul(matmul(tri_factor.T, inner_gram), tri_factor)
    middle_sym = 0.5 * (middle + middle.T)
    left = jnp.concatenate([refl_rows, -matmul(refl_rows, middle_sym)], axis=1)
    right_cols = jnp.concatenate([update_cols, refl_cols], axis=1)
    updated = partial - matmul_nt_fast(left, right_cols)
    return (updated, -chol_t)


def solution(mesh):
    return jax.shard_map(
        shards,
        mesh=mesh,
        in_specs=(P("row", "col"), P("row", None)),
        out_specs=(P("row", "col"), P()),
        check_vma=False,
    )
```

```python
import jax
import jax.numpy as jnp
from jax import lax
from jax.experimental import pallas as pl
from jax.sharding import PartitionSpec as P

_INTERPRET = False
_CHUNK = 16


def matmul(left, right):
    return jnp.dot(left, right, precision=lax.Precision.HIGHEST, preferred_element_type=jnp.float32)


def matmul_tn(left, right):
    return lax.dot_general(
        left,
        right,
        (((0,), (0,)), ((), ())),
        precision=lax.Precision.HIGHEST,
        preferred_element_type=jnp.float32,
    )


def matmul_nt(left, right):
    return lax.dot_general(
        left,
        right,
        (((1,), (1,)), ((), ())),
        precision=lax.Precision.HIGHEST,
        preferred_element_type=jnp.float32,
    )


def _elim_kernel(m_ref, f_ref, r_ref):
    count, n, _ = m_ref.shape
    f_ref[...] = m_ref[...]
    ri = lax.broadcasted_iota(jnp.int32, (n, n), 0)
    ci = lax.broadcasted_iota(jnp.int32, (n, n), 1)
    for b in range(count):
        r_ref[b] = jnp.where(ri == ci, 1.0, 0.0).astype(jnp.float32)
    for chunk in range(n // _CHUNK):
        r0 = chunk * _CHUNK
        c0 = (r0 // 128) * 128
        rc1 = min(n, ((r0 + _CHUNK - 1) // 128 + 1) * 128)
        nr = n - r0
        nc = n - c0

        def step(j, carry, r0=r0, c0=c0, rc1=rc1, nr=nr, nc=nc):
            rows = lax.broadcasted_iota(jnp.int32, (nr, nc), 0) + r0
            lanes = lax.broadcasted_iota(jnp.int32, (nr, nc), 1) + c0
            lanes_row = lax.broadcasted_iota(jnp.int32, (1, nc), 1) + c0
            rows_col = lax.broadcasted_iota(jnp.int32, (nr, 1), 0) + r0
            r_rows = lax.broadcasted_iota(jnp.int32, (_CHUNK, rc1), 0) + r0
            for b in range(count):
                f = f_ref[b, r0:, c0:]
                row_j = jnp.sum(jnp.where(rows[:_CHUNK] == j, f[:_CHUNK], 0.0), axis=0, keepdims=True)
                col_j = jnp.sum(jnp.where(lanes == j, f, 0.0), axis=1, keepdims=True)
                pivot = jnp.sum(jnp.where(lanes_row == j, row_j, 0.0), axis=1, keepdims=True)
                mult = jnp.where(rows_col > j, col_j / pivot, 0.0)
                upd = jnp.where(lanes_row > j, row_j, 0.0)
                f = f - mult * upd
                f = jnp.where((lanes == j) & (rows > j), mult, f)
                f_ref[b, r0:, c0:] = f
                r_now = r_ref[b, r0:, :rc1]
                r_row = jnp.sum(jnp.where(r_rows == j, r_now[:_CHUNK], 0.0), axis=0, keepdims=True)
                r_ref[b, r0:, :rc1] = r_now - mult * r_row
            return carry

        lax.fori_loop(r0, r0 + _CHUNK, step, 0)


def eliminate(stack):
    return pl.pallas_call(
        _elim_kernel,
        out_shape=[jax.ShapeDtypeStruct(stack.shape, jnp.float32)] * 2,
        interpret=_INTERPRET,
    )(stack)


def matmul_fast(left, right):
    return jnp.dot(left, right, precision=lax.Precision.HIGH, preferred_element_type=jnp.float32)


def matmul_tn_fast(left, right):
    return lax.dot_general(
        left,
        right,
        (((0,), (0,)), ((), ())),
        precision=lax.Precision.HIGH,
        preferred_element_type=jnp.float32,
    )


def matmul_nt_fast(left, right):
    return lax.dot_general(
        left,
        right,
        (((1,), (1,)), ((), ())),
        precision=lax.Precision.HIGH,
        preferred_element_type=jnp.float32,
    )


def _xor_pairs(count, bit):
    return [(i, i ^ bit) for i in range(count)]


def psum_doubling(value, axis):
    count = lax.axis_size(axis)
    bit = 1
    while bit < count:
        value = value + lax.ppermute(value, axis, _xor_pairs(count, bit))
        bit *= 2
    return value


def _rotations(bits, chunks):
    return [bits[i % len(bits):] + bits[:i % len(bits)] for i in range(chunks)]


def psum_doubling_rot(value, axis, bits, chunks):
    parts = jnp.split(value, chunks)
    count = lax.axis_size(axis)
    out = []
    for part, order in zip(parts, _rotations(bits, chunks)):
        for bit in order:
            part = part + lax.ppermute(part, axis, _xor_pairs(count, bit))
        out.append(part)
    return jnp.concatenate(out)


def _halving(keep, axis, bits, index, count, tie=None):
    for bit in bits:
        half = keep.shape[0] // 2
        upper = (index & bit) != 0
        send = jnp.where(upper, keep[:half], keep[half:])
        mine = jnp.where(upper, keep[half:], keep[:half])
        keep = mine + lax.ppermute(send, axis, _xor_pairs(count, bit))
    for bit in reversed(bits):
        if bit == bits[0] and tie is not None:
            keep, tie = lax.optimization_barrier((keep, tie))
        upper = (index & bit) != 0
        other = lax.ppermute(keep, axis, _xor_pairs(count, bit))
        keep = jnp.where(upper, jnp.concatenate([other, keep]), jnp.concatenate([keep, other]))
    if tie is not None:
        return keep, tie
    return keep


def psum_halving(value, axis, bits, chunks):
    index = lax.axis_index(axis)
    count = lax.axis_size(axis)
    parts = jnp.split(value, chunks)
    out = [_halving(part, axis, order, index, count) for part, order in zip(parts, _rotations(bits, chunks))]
    return jnp.concatenate(out)


def mirror_tree(row_piece, band_size):
    row_count = lax.axis_size("row")
    col_count = lax.axis_size("col")
    assert row_count == 2 * col_count
    row_index = lax.axis_index("row")
    col_index = lax.axis_index("col")
    piece = row_piece
    bit = 1
    while bit < col_count:
        pairs = []
        receivers = []
        for c in range(col_count):
            for r in range(row_count):
                if ((r ^ c) & (col_count - 1)) & ~(bit - 1) == 0:
                    pairs.append((r * col_count + c, (r ^ bit) * col_count + c))
                    receivers.append((r ^ bit) * col_count + c)
        received = lax.ppermute(piece, ("row", "col"), pairs)
        me = row_index * col_count + col_index
        is_receiver = jnp.zeros((), jnp.bool_)
        for dev in receivers:
            is_receiver = is_receiver | (me == dev)
        piece = jnp.where(is_receiver, received, piece)
        bit *= 2
    other = lax.ppermute(piece, "row", _xor_pairs(row_count, col_count))
    high = row_index >= col_count
    first = jnp.where(high, other, piece)
    second = jnp.where(high, piece, other)
    blocks = row_piece.shape[0] // band_size
    stacked = jnp.stack([first, second]).reshape(2, blocks, band_size, row_piece.shape[1])
    return stacked.transpose(1, 0, 2, 3).reshape(2 * row_piece.shape[0], row_piece.shape[1])


def small_factors(gram_total, top_rows):
    band_size = gram_total.shape[0]
    identity = jnp.eye(band_size, dtype=jnp.float32)
    gram_f, gram_r = eliminate(gram_total[None])
    gram_f = gram_f[0]
    scale = 1.0 / jnp.sqrt(jnp.diagonal(gram_f))
    chol_t = scale[:, None] * jnp.triu(gram_f)
    chol_inverse = scale[:, None] * gram_r[0]
    ortho_top = matmul_nt(top_rows, chol_inverse)
    shifted_top = identity + ortho_top
    lu_f, lu_r = eliminate(jnp.stack([shifted_top, shifted_top.T]))
    upper_tri = jnp.triu(lu_f[0])
    unit_inverse = lu_r[0]
    upper_inverse = lu_r[1].T / jnp.diagonal(lu_f[1])[None, :]
    tri_factor = matmul_nt(upper_tri, unit_inverse)
    right = matmul_tn(chol_inverse, upper_inverse)
    return chol_t, right, upper_inverse, tri_factor


def shards(trailing, panel):
    row_index = lax.axis_index("row")
    col_index = lax.axis_index("col")
    band_size = panel.shape[1]
    row_bits = tuple(1 << i for i in range(lax.axis_size("row").bit_length() - 1))
    col_bits = tuple(1 << i for i in range(lax.axis_size("col").bit_length() - 1))
    first_owner = (row_index == 0).astype(jnp.float32)
    first_col = (col_index == 0).astype(jnp.float32)
    gram_part = matmul_tn(panel, panel)
    top_part = panel[:band_size] * first_owner
    panel_cols = mirror_tree(panel, band_size)
    stacked = psum_halving(jnp.concatenate([gram_part, top_part]), "row", row_bits, 1)
    gram_total = stacked[:band_size]
    top_rows = stacked[band_size:]
    cols_part = jnp.concatenate(
        [matmul_tn_fast(trailing, panel), trailing[:band_size].T * first_owner], axis=1)
    cols_part, gram_total = lax.optimization_barrier((cols_part, gram_total))
    cols_sums = psum_halving(cols_part, "row", row_bits, 1)
    rows_part = jnp.concatenate(
        [matmul_fast(trailing, panel_cols), trailing[:, :band_size] * first_col], axis=1)
    rows_sums = psum_halving(rows_part, "col", col_bits, 1)
    chol_t, right, upper_inverse, tri_factor = small_factors(gram_total, top_rows)
    refl_rows = matmul(panel, right)
    refl_rows = refl_rows.at[:band_size].add(upper_inverse * first_owner)
    refl_cols = matmul(panel_cols, right)
    refl_cols = refl_cols.at[:band_size].add(upper_inverse * first_col)
    product_rows = matmul(rows_sums[:, :band_size], right) + matmul(rows_sums[:, band_size:], upper_inverse)
    product_cols = matmul(cols_sums[:, :band_size], right) + matmul(cols_sums[:, band_size:], upper_inverse)
    inner_gram = psum_doubling_rot(matmul_tn(refl_rows, product_rows), "row", row_bits, 1)
    update_rows = matmul(product_rows, tri_factor)
    partial = trailing - matmul_nt_fast(update_rows, refl_cols)
    update_cols = matmul(product_cols, tri_factor)
    middle = matmul(matmul(tri_factor.T, inner_gram), tri_factor)
    middle_sym = 0.5 * (middle + middle.T)
    left = jnp.concatenate([refl_rows, -matmul(refl_rows, middle_sym)], axis=1)
    right_cols = jnp.concatenate([update_cols, refl_cols], axis=1)
    updated = partial - matmul_nt_fast(left, right_cols)
    return (updated, -chol_t)


def solution(mesh):
    return jax.shard_map(
        shards,
        mesh=mesh,
        in_specs=(P("row", "col"), P("row", None)),
        out_specs=(P("row", "col"), P()),
        check_vma=False,
    )
```

```python
import jax
import jax.numpy as jnp
from jax import lax
from jax.experimental import pallas as pl
from jax.sharding import PartitionSpec as P

_INTERPRET = False
_CHUNK = 16


def matmul(left, right):
    return jnp.dot(left, right, precision=lax.Precision.HIGHEST, preferred_element_type=jnp.float32)


def matmul_tn(left, right):
    return lax.dot_general(
        left,
        right,
        (((0,), (0,)), ((), ())),
        precision=lax.Precision.HIGHEST,
        preferred_element_type=jnp.float32,
    )


def matmul_nt(left, right):
    return lax.dot_general(
        left,
        right,
        (((1,), (1,)), ((), ())),
        precision=lax.Precision.HIGHEST,
        preferred_element_type=jnp.float32,
    )


def _elim_kernel(m_ref, f_ref, r_ref):
    count, n, _ = m_ref.shape
    f_ref[...] = m_ref[...]
    ri = lax.broadcasted_iota(jnp.int32, (n, n), 0)
    ci = lax.broadcasted_iota(jnp.int32, (n, n), 1)
    for b in range(count):
        r_ref[b] = jnp.where(ri == ci, 1.0, 0.0).astype(jnp.float32)
    for chunk in range(n // _CHUNK):
        r0 = chunk * _CHUNK
        c0 = (r0 // 128) * 128
        rc1 = min(n, ((r0 + _CHUNK - 1) // 128 + 1) * 128)
        nr = n - r0
        nc = n - c0

        def step(j, carry, r0=r0, c0=c0, rc1=rc1, nr=nr, nc=nc):
            rows = lax.broadcasted_iota(jnp.int32, (nr, nc), 0) + r0
            lanes = lax.broadcasted_iota(jnp.int32, (nr, nc), 1) + c0
            lanes_row = lax.broadcasted_iota(jnp.int32, (1, nc), 1) + c0
            rows_col = lax.broadcasted_iota(jnp.int32, (nr, 1), 0) + r0
            r_rows = lax.broadcasted_iota(jnp.int32, (_CHUNK, rc1), 0) + r0
            for b in range(count):
                f = f_ref[b, r0:, c0:]
                row_j = jnp.sum(jnp.where(rows[:_CHUNK] == j, f[:_CHUNK], 0.0), axis=0, keepdims=True)
                col_j = jnp.sum(jnp.where(lanes == j, f, 0.0), axis=1, keepdims=True)
                pivot = jnp.sum(jnp.where(lanes_row == j, row_j, 0.0), axis=1, keepdims=True)
                mult = jnp.where(rows_col > j, col_j / pivot, 0.0)
                upd = jnp.where(lanes_row > j, row_j, 0.0)
                f = f - mult * upd
                f = jnp.where((lanes == j) & (rows > j), mult, f)
                f_ref[b, r0:, c0:] = f
                r_now = r_ref[b, r0:, :rc1]
                r_row = jnp.sum(jnp.where(r_rows == j, r_now[:_CHUNK], 0.0), axis=0, keepdims=True)
                r_ref[b, r0:, :rc1] = r_now - mult * r_row
            return carry

        lax.fori_loop(r0, r0 + _CHUNK, step, 0)


def eliminate(stack):
    return pl.pallas_call(
        _elim_kernel,
        out_shape=[jax.ShapeDtypeStruct(stack.shape, jnp.float32)] * 2,
        interpret=_INTERPRET,
    )(stack)


def matmul_fast(left, right):
    return jnp.dot(left, right, precision=lax.Precision.HIGH, preferred_element_type=jnp.float32)


def matmul_tn_fast(left, right):
    return lax.dot_general(
        left,
        right,
        (((0,), (0,)), ((), ())),
        precision=lax.Precision.HIGH,
        preferred_element_type=jnp.float32,
    )


def matmul_nt_fast(left, right):
    return lax.dot_general(
        left,
        right,
        (((1,), (1,)), ((), ())),
        precision=lax.Precision.HIGH,
        preferred_element_type=jnp.float32,
    )


def _xor_pairs(count, bit):
    return [(i, i ^ bit) for i in range(count)]


def psum_doubling(value, axis):
    count = lax.axis_size(axis)
    bit = 1
    while bit < count:
        value = value + lax.ppermute(value, axis, _xor_pairs(count, bit))
        bit *= 2
    return value


def _rotations(bits, chunks):
    return [bits[i % len(bits):] + bits[:i % len(bits)] for i in range(chunks)]


def psum_doubling_rot(value, axis, bits, chunks):
    parts = jnp.split(value, chunks)
    count = lax.axis_size(axis)
    out = []
    for part, order in zip(parts, _rotations(bits, chunks)):
        for bit in order:
            part = part + lax.ppermute(part, axis, _xor_pairs(count, bit))
        out.append(part)
    return jnp.concatenate(out)


def _halving(keep, axis, bits, index, count, tie=None):
    for bit in bits:
        half = keep.shape[0] // 2
        upper = (index & bit) != 0
        send = jnp.where(upper, keep[:half], keep[half:])
        mine = jnp.where(upper, keep[half:], keep[:half])
        keep = mine + lax.ppermute(send, axis, _xor_pairs(count, bit))
    for bit in reversed(bits):
        if bit == bits[0] and tie is not None:
            keep, tie = lax.optimization_barrier((keep, tie))
        upper = (index & bit) != 0
        other = lax.ppermute(keep, axis, _xor_pairs(count, bit))
        keep = jnp.where(upper, jnp.concatenate([other, keep]), jnp.concatenate([keep, other]))
    if tie is not None:
        return keep, tie
    return keep


def psum_halving(value, axis, bits, chunks):
    index = lax.axis_index(axis)
    count = lax.axis_size(axis)
    parts = jnp.split(value, chunks)
    out = [_halving(part, axis, order, index, count) for part, order in zip(parts, _rotations(bits, chunks))]
    return jnp.concatenate(out)


def mirror_tree(row_piece, band_size):
    row_count = lax.axis_size("row")
    col_count = lax.axis_size("col")
    assert row_count == 2 * col_count
    row_index = lax.axis_index("row")
    col_index = lax.axis_index("col")
    piece = row_piece
    bit = 1
    while bit < col_count:
        pairs = []
        receivers = []
        for c in range(col_count):
            for r in range(row_count):
                if ((r ^ c) & (col_count - 1)) & ~(bit - 1) == 0:
                    pairs.append((r * col_count + c, (r ^ bit) * col_count + c))
                    receivers.append((r ^ bit) * col_count + c)
        received = lax.ppermute(piece, ("row", "col"), pairs)
        me = row_index * col_count + col_index
        is_receiver = jnp.zeros((), jnp.bool_)
        for dev in receivers:
            is_receiver = is_receiver | (me == dev)
        piece = jnp.where(is_receiver, received, piece)
        bit *= 2
    other = lax.ppermute(piece, "row", _xor_pairs(row_count, col_count))
    high = row_index >= col_count
    first = jnp.where(high, other, piece)
    second = jnp.where(high, piece, other)
    blocks = row_piece.shape[0] // band_size
    stacked = jnp.stack([first, second]).reshape(2, blocks, band_size, row_piece.shape[1])
    return stacked.transpose(1, 0, 2, 3).reshape(2 * row_piece.shape[0], row_piece.shape[1])


def _diagonal(matrix):
    rows = lax.broadcasted_iota(jnp.int32, matrix.shape, 0)
    cols = lax.broadcasted_iota(jnp.int32, matrix.shape, 1)
    return jnp.sum(jnp.where(rows == cols, matrix, 0.0), axis=0)


def small_factors(gram_total, top_rows):
    band_size = gram_total.shape[0]
    identity = jnp.eye(band_size, dtype=jnp.float32)
    gram_f, gram_r = eliminate(gram_total[None])
    gram_f = gram_f[0]
    scale = 1.0 / jnp.sqrt(_diagonal(gram_f))
    chol_t = scale[:, None] * jnp.triu(gram_f)
    chol_inverse = scale[:, None] * gram_r[0]
    ortho_top = matmul_nt(top_rows, chol_inverse)
    shifted_top = identity + ortho_top
    lu_f, lu_r = eliminate(jnp.stack([shifted_top, shifted_top.T]))
    upper_tri = jnp.triu(lu_f[0])
    unit_inverse = lu_r[0]
    upper_inverse = lu_r[1].T / _diagonal(lu_f[1])[None, :]
    tri_factor = matmul_nt(upper_tri, unit_inverse)
    right = matmul_tn(chol_inverse, upper_inverse)
    return chol_t, right, upper_inverse, tri_factor


def shards(trailing, panel):
    row_index = lax.axis_index("row")
    col_index = lax.axis_index("col")
    band_size = panel.shape[1]
    row_bits = tuple(1 << i for i in range(lax.axis_size("row").bit_length() - 1))
    col_bits = tuple(1 << i for i in range(lax.axis_size("col").bit_length() - 1))
    first_owner = (row_index == 0).astype(jnp.float32)
    first_col = (col_index == 0).astype(jnp.float32)
    gram_part = matmul_tn(panel, panel)
    top_part = panel[:band_size] * first_owner
    panel_cols = mirror_tree(panel, band_size)
    stacked = psum_halving(jnp.concatenate([gram_part, top_part]), "row", row_bits, 1)
    gram_total = stacked[:band_size]
    top_rows = stacked[band_size:]
    chol_t, right, upper_inverse, tri_factor = small_factors(gram_total, top_rows)
    refl_rows = matmul_fast(panel, right)
    refl_rows = refl_rows.at[:band_size].add(upper_inverse * first_owner)
    refl_cols = matmul_fast(panel_cols, right)
    refl_cols = refl_cols.at[:band_size].add(upper_inverse * first_col)
    product_rows = psum_halving(matmul_fast(trailing, refl_cols), "col", col_bits, 1)
    inner_gram = psum_doubling_rot(matmul_tn(refl_rows, product_rows), "row", row_bits, 1)
    update_rows = matmul_fast(product_rows, tri_factor)
    partial = trailing - matmul_nt_fast(update_rows, refl_cols)
    index = lax.axis_index("row")
    count = lax.axis_size("row")
    product_cols, partial = _halving(matmul_tn_fast(trailing, refl_rows), "row", row_bits, index, count, partial)
    update_cols = matmul_fast(product_cols, tri_factor)
    middle = matmul(matmul(tri_factor.T, inner_gram), tri_factor)
    middle_sym = 0.5 * (middle + middle.T)
    left = jnp.concatenate([refl_rows, -matmul(refl_rows, middle_sym)], axis=1)
    right_cols = jnp.concatenate([update_cols, refl_cols], axis=1)
    updated = partial - matmul_nt_fast(left, right_cols)
    return (updated, -chol_t)


def solution(mesh):
    return jax.shard_map(
        shards,
        mesh=mesh,
        in_specs=(P("row", "col"), P("row", None)),
        out_specs=(P("row", "col"), P()),
        check_vma=False,
    )
```

```python
import jax
import jax.numpy as jnp
from jax import lax
from jax.experimental import pallas as pl
from jax.sharding import PartitionSpec as P

_INTERPRET = False
_CHUNK = 16


def matmul(left, right):
    return jnp.dot(left, right, precision=lax.Precision.HIGHEST, preferred_element_type=jnp.float32)


def matmul_tn(left, right):
    return lax.dot_general(
        left,
        right,
        (((0,), (0,)), ((), ())),
        precision=lax.Precision.HIGHEST,
        preferred_element_type=jnp.float32,
    )


def matmul_nt(left, right):
    return lax.dot_general(
        left,
        right,
        (((1,), (1,)), ((), ())),
        precision=lax.Precision.HIGHEST,
        preferred_element_type=jnp.float32,
    )


def _elim_kernel(m_ref, f_ref, r_ref):
    count, n, _ = m_ref.shape
    f_ref[...] = m_ref[...]
    ri = lax.broadcasted_iota(jnp.int32, (n, n), 0)
    ci = lax.broadcasted_iota(jnp.int32, (n, n), 1)
    for b in range(count):
        r_ref[b] = jnp.where(ri == ci, 1.0, 0.0).astype(jnp.float32)
    for chunk in range(n // _CHUNK):
        r0 = chunk * _CHUNK
        c0 = (r0 // 128) * 128
        rc1 = min(n, ((r0 + _CHUNK - 1) // 128 + 1) * 128)
        nr = n - r0
        nc = n - c0

        def step(j, carry, r0=r0, c0=c0, rc1=rc1, nr=nr, nc=nc):
            rows = lax.broadcasted_iota(jnp.int32, (nr, nc), 0) + r0
            lanes = lax.broadcasted_iota(jnp.int32, (nr, nc), 1) + c0
            lanes_row = lax.broadcasted_iota(jnp.int32, (1, nc), 1) + c0
            rows_col = lax.broadcasted_iota(jnp.int32, (nr, 1), 0) + r0
            r_rows = lax.broadcasted_iota(jnp.int32, (_CHUNK, rc1), 0) + r0
            for b in range(count):
                f = f_ref[b, r0:, c0:]
                row_j = jnp.sum(jnp.where(rows[:_CHUNK] == j, f[:_CHUNK], 0.0), axis=0, keepdims=True)
                col_j = jnp.sum(jnp.where(lanes == j, f, 0.0), axis=1, keepdims=True)
                pivot = jnp.sum(jnp.where(lanes_row == j, row_j, 0.0), axis=1, keepdims=True)
                mult = jnp.where(rows_col > j, col_j / pivot, 0.0)
                upd = jnp.where(lanes_row > j, row_j, 0.0)
                f = f - mult * upd
                f = jnp.where((lanes == j) & (rows > j), mult, f)
                f_ref[b, r0:, c0:] = f
                r_now = r_ref[b, r0:, :rc1]
                r_row = jnp.sum(jnp.where(r_rows == j, r_now[:_CHUNK], 0.0), axis=0, keepdims=True)
                r_ref[b, r0:, :rc1] = r_now - mult * r_row
            return carry

        lax.fori_loop(r0, r0 + _CHUNK, step, 0)


def eliminate(stack):
    return pl.pallas_call(
        _elim_kernel,
        out_shape=[jax.ShapeDtypeStruct(stack.shape, jnp.float32)] * 2,
        interpret=_INTERPRET,
    )(stack)


def matmul_fast(left, right):
    return jnp.dot(left, right, precision=lax.Precision.HIGH, preferred_element_type=jnp.float32)


def matmul_tn_fast(left, right):
    return lax.dot_general(
        left,
        right,
        (((0,), (0,)), ((), ())),
        precision=lax.Precision.HIGH,
        preferred_element_type=jnp.float32,
    )


def matmul_nt_fast(left, right):
    return lax.dot_general(
        left,
        right,
        (((1,), (1,)), ((), ())),
        precision=lax.Precision.HIGH,
        preferred_element_type=jnp.float32,
    )


def _xor_pairs(count, bit):
    return [(i, i ^ bit) for i in range(count)]


def psum_doubling(value, axis):
    count = lax.axis_size(axis)
    bit = 1
    while bit < count:
        value = value + lax.ppermute(value, axis, _xor_pairs(count, bit))
        bit *= 2
    return value


def _rotations(bits, chunks):
    return [bits[i % len(bits):] + bits[:i % len(bits)] for i in range(chunks)]


def psum_doubling_rot(value, axis, bits, chunks):
    parts = jnp.split(value, chunks)
    count = lax.axis_size(axis)
    out = []
    for part, order in zip(parts, _rotations(bits, chunks)):
        for bit in order:
            part = part + lax.ppermute(part, axis, _xor_pairs(count, bit))
        out.append(part)
    return jnp.concatenate(out)


def _halving(keep, axis, bits, index, count, tie=None):
    for bit in bits:
        half = keep.shape[0] // 2
        upper = (index & bit) != 0
        send = jnp.where(upper, keep[:half], keep[half:])
        mine = jnp.where(upper, keep[half:], keep[:half])
        keep = mine + lax.ppermute(send, axis, _xor_pairs(count, bit))
    for bit in reversed(bits):
        if bit == bits[0] and tie is not None:
            keep, tie = lax.optimization_barrier((keep, tie))
        upper = (index & bit) != 0
        other = lax.ppermute(keep, axis, _xor_pairs(count, bit))
        keep = jnp.where(upper, jnp.concatenate([other, keep]), jnp.concatenate([keep, other]))
    if tie is not None:
        return keep, tie
    return keep


def psum_halving(value, axis, bits, chunks):
    index = lax.axis_index(axis)
    count = lax.axis_size(axis)
    parts = jnp.split(value, chunks)
    out = [_halving(part, axis, order, index, count) for part, order in zip(parts, _rotations(bits, chunks))]
    return jnp.concatenate(out)


def mirror_tree(row_piece, band_size):
    row_count = lax.axis_size("row")
    col_count = lax.axis_size("col")
    assert row_count == 2 * col_count
    row_index = lax.axis_index("row")
    col_index = lax.axis_index("col")
    piece = row_piece
    bit = 1
    while bit < col_count:
        pairs = []
        receivers = []
        for c in range(col_count):
            for r in range(row_count):
                if ((r ^ c) & (col_count - 1)) & ~(bit - 1) == 0:
                    pairs.append((r * col_count + c, (r ^ bit) * col_count + c))
                    receivers.append((r ^ bit) * col_count + c)
        received = lax.ppermute(piece, ("row", "col"), pairs)
        me = row_index * col_count + col_index
        is_receiver = jnp.zeros((), jnp.bool_)
        for dev in receivers:
            is_receiver = is_receiver | (me == dev)
        piece = jnp.where(is_receiver, received, piece)
        bit *= 2
    other = lax.ppermute(piece, "row", _xor_pairs(row_count, col_count))
    high = row_index >= col_count
    first = jnp.where(high, other, piece)
    second = jnp.where(high, piece, other)
    blocks = row_piece.shape[0] // band_size
    stacked = jnp.stack([first, second]).reshape(2, blocks, band_size, row_piece.shape[1])
    return stacked.transpose(1, 0, 2, 3).reshape(2 * row_piece.shape[0], row_piece.shape[1])


def _diagonal(matrix):
    rows = lax.broadcasted_iota(jnp.int32, matrix.shape, 0)
    cols = lax.broadcasted_iota(jnp.int32, matrix.shape, 1)
    return jnp.sum(jnp.where(rows == cols, matrix, 0.0), axis=0)


def small_factors(gram_total, top_rows):
    band_size = gram_total.shape[0]
    identity = jnp.eye(band_size, dtype=jnp.float32)
    gram_f, gram_r = eliminate(gram_total[None])
    gram_f = gram_f[0]
    scale = 1.0 / jnp.sqrt(_diagonal(gram_f))
    chol_t = scale[:, None] * jnp.triu(gram_f)
    chol_inverse = scale[:, None] * gram_r[0]
    ortho_top = matmul_nt(top_rows, chol_inverse)
    shifted_top = identity + ortho_top
    lu_f, lu_r = eliminate(jnp.stack([shifted_top, shifted_top.T]))
    upper_tri = jnp.triu(lu_f[0])
    unit_inverse = lu_r[0]
    upper_inverse = lu_r[1].T / _diagonal(lu_f[1])[None, :]
    tri_factor = matmul_nt(upper_tri, unit_inverse)
    right = matmul_tn(chol_inverse, upper_inverse)
    return chol_t, right, upper_inverse, tri_factor


def shards(trailing, panel):
    row_index = lax.axis_index("row")
    col_index = lax.axis_index("col")
    band_size = panel.shape[1]
    row_bits = tuple(1 << i for i in range(lax.axis_size("row").bit_length() - 1))
    col_bits = tuple(1 << i for i in range(lax.axis_size("col").bit_length() - 1))
    first_owner = (row_index == 0).astype(jnp.float32)
    first_col = (col_index == 0).astype(jnp.float32)
    gram_part = matmul_tn(panel, panel)
    top_part = panel[:band_size] * first_owner
    panel_cols = mirror_tree(panel, band_size)
    stacked = psum_halving(jnp.concatenate([gram_part, top_part]), "row", row_bits, 1)
    gram_total = stacked[:band_size]
    top_rows = stacked[band_size:]
    chol_t, right, upper_inverse, tri_factor = small_factors(gram_total, top_rows)
    refl_rows = matmul_fast(panel, right)
    refl_rows = refl_rows.at[:band_size].add(upper_inverse * first_owner)
    refl_cols = matmul_fast(panel_cols, right)
    refl_cols = refl_cols.at[:band_size].add(upper_inverse * first_col)
    product_rows = psum_halving(matmul_fast(trailing, refl_cols), "col", col_bits, 1)
    inner_gram = psum_doubling_rot(matmul_tn(refl_rows, product_rows), "row", row_bits[::-1], 1)
    update_rows = matmul_fast(product_rows, tri_factor)
    partial = trailing - matmul_nt_fast(update_rows, refl_cols)
    index = lax.axis_index("row")
    count = lax.axis_size("row")
    product_cols, partial = _halving(matmul_tn_fast(trailing, refl_rows), "row", row_bits, index, count, partial)
    update_cols = matmul_fast(product_cols, tri_factor)
    middle = matmul(matmul(tri_factor.T, inner_gram), tri_factor)
    middle_sym = 0.5 * (middle + middle.T)
    left = jnp.concatenate([refl_rows, -matmul(refl_rows, middle_sym)], axis=1)
    right_cols = jnp.concatenate([update_cols, refl_cols], axis=1)
    updated = partial - matmul_nt_fast(left, right_cols)
    return (updated, -chol_t)


def solution(mesh):
    return jax.shard_map(
        shards,
        mesh=mesh,
        in_specs=(P("row", "col"), P("row", None)),
        out_specs=(P("row", "col"), P()),
        check_vma=False,
    )
```

```python
import jax
import jax.numpy as jnp
from jax import lax
from jax.experimental import pallas as pl
from jax.sharding import PartitionSpec as P

_INTERPRET = False
_CHUNK = 16


def matmul(left, right):
    return jnp.dot(left, right, precision=lax.Precision.HIGHEST, preferred_element_type=jnp.float32)


def matmul_tn(left, right):
    return lax.dot_general(
        left,
        right,
        (((0,), (0,)), ((), ())),
        precision=lax.Precision.HIGHEST,
        preferred_element_type=jnp.float32,
    )


def matmul_nt(left, right):
    return lax.dot_general(
        left,
        right,
        (((1,), (1,)), ((), ())),
        precision=lax.Precision.HIGHEST,
        preferred_element_type=jnp.float32,
    )


def _elim_kernel(m_ref, f_ref, r_ref):
    count, n, _ = m_ref.shape
    f_ref[...] = m_ref[...]
    ri = lax.broadcasted_iota(jnp.int32, (n, n), 0)
    ci = lax.broadcasted_iota(jnp.int32, (n, n), 1)
    for b in range(count):
        r_ref[b] = jnp.where(ri == ci, 1.0, 0.0).astype(jnp.float32)
    for chunk in range(n // _CHUNK):
        r0 = chunk * _CHUNK
        c0 = (r0 // 128) * 128
        rc1 = min(n, ((r0 + _CHUNK - 1) // 128 + 1) * 128)
        nr = n - r0
        nc = n - c0

        def step(j, carry, r0=r0, c0=c0, rc1=rc1, nr=nr, nc=nc):
            rows = lax.broadcasted_iota(jnp.int32, (nr, nc), 0) + r0
            lanes = lax.broadcasted_iota(jnp.int32, (nr, nc), 1) + c0
            lanes_row = lax.broadcasted_iota(jnp.int32, (1, nc), 1) + c0
            rows_col = lax.broadcasted_iota(jnp.int32, (nr, 1), 0) + r0
            r_rows = lax.broadcasted_iota(jnp.int32, (_CHUNK, rc1), 0) + r0
            for b in range(count):
                f = f_ref[b, r0:, c0:]
                row_j = jnp.sum(jnp.where(rows[:_CHUNK] == j, f[:_CHUNK], 0.0), axis=0, keepdims=True)
                col_j = jnp.sum(jnp.where(lanes == j, f, 0.0), axis=1, keepdims=True)
                pivot = jnp.sum(jnp.where(lanes_row == j, row_j, 0.0), axis=1, keepdims=True)
                mult = jnp.where(rows_col > j, col_j / pivot, 0.0)
                upd = jnp.where(lanes_row > j, row_j, 0.0)
                f = f - mult * upd
                f = jnp.where((lanes == j) & (rows > j), mult, f)
                f_ref[b, r0:, c0:] = f
                r_now = r_ref[b, r0:, :rc1]
                r_row = jnp.sum(jnp.where(r_rows == j, r_now[:_CHUNK], 0.0), axis=0, keepdims=True)
                r_ref[b, r0:, :rc1] = r_now - mult * r_row
            return carry

        lax.fori_loop(r0, r0 + _CHUNK, step, 0)


def eliminate(stack):
    return pl.pallas_call(
        _elim_kernel,
        out_shape=[jax.ShapeDtypeStruct(stack.shape, jnp.float32)] * 2,
        interpret=_INTERPRET,
    )(stack)


def matmul_fast(left, right):
    return jnp.dot(left, right, precision=lax.Precision.HIGH, preferred_element_type=jnp.float32)


def matmul_tn_fast(left, right):
    return lax.dot_general(
        left,
        right,
        (((0,), (0,)), ((), ())),
        precision=lax.Precision.HIGH,
        preferred_element_type=jnp.float32,
    )


def matmul_nt_fast(left, right):
    return lax.dot_general(
        left,
        right,
        (((1,), (1,)), ((), ())),
        precision=lax.Precision.HIGH,
        preferred_element_type=jnp.float32,
    )


def _xor_pairs(count, bit):
    return [(i, i ^ bit) for i in range(count)]


def psum_doubling(value, axis):
    count = lax.axis_size(axis)
    bit = 1
    while bit < count:
        value = value + lax.ppermute(value, axis, _xor_pairs(count, bit))
        bit *= 2
    return value


def _rotations(bits, chunks):
    return [bits[i % len(bits):] + bits[:i % len(bits)] for i in range(chunks)]


def psum_doubling_rot(value, axis, bits, chunks):
    parts = jnp.split(value, chunks)
    count = lax.axis_size(axis)
    out = []
    for part, order in zip(parts, _rotations(bits, chunks)):
        for bit in order:
            part = part + lax.ppermute(part, axis, _xor_pairs(count, bit))
        out.append(part)
    return jnp.concatenate(out)


def _halving(keep, axis, bits, index, count, tie=None):
    for bit in bits:
        half = keep.shape[0] // 2
        upper = (index & bit) != 0
        send = jnp.where(upper, keep[:half], keep[half:])
        mine = jnp.where(upper, keep[half:], keep[:half])
        keep = mine + lax.ppermute(send, axis, _xor_pairs(count, bit))
    for bit in reversed(bits):
        if bit == bits[0] and tie is not None:
            keep, tie = lax.optimization_barrier((keep, tie))
        upper = (index & bit) != 0
        other = lax.ppermute(keep, axis, _xor_pairs(count, bit))
        keep = jnp.where(upper, jnp.concatenate([other, keep]), jnp.concatenate([keep, other]))
    if tie is not None:
        return keep, tie
    return keep


def psum_halving(value, axis, bits, chunks):
    index = lax.axis_index(axis)
    count = lax.axis_size(axis)
    parts = jnp.split(value, chunks)
    out = [_halving(part, axis, order, index, count) for part, order in zip(parts, _rotations(bits, chunks))]
    return jnp.concatenate(out)


def mirror_tree(row_piece, band_size):
    row_count = lax.axis_size("row")
    col_count = lax.axis_size("col")
    assert row_count == 2 * col_count
    row_index = lax.axis_index("row")
    col_index = lax.axis_index("col")
    piece = row_piece
    bit = 1
    while bit < col_count:
        pairs = []
        receivers = []
        for c in range(col_count):
            for r in range(row_count):
                if ((r ^ c) & (col_count - 1)) & ~(bit - 1) == 0:
                    pairs.append((r * col_count + c, (r ^ bit) * col_count + c))
                    receivers.append((r ^ bit) * col_count + c)
        received = lax.ppermute(piece, ("row", "col"), pairs)
        me = row_index * col_count + col_index
        is_receiver = jnp.zeros((), jnp.bool_)
        for dev in receivers:
            is_receiver = is_receiver | (me == dev)
        piece = jnp.where(is_receiver, received, piece)
        bit *= 2
    other = lax.ppermute(piece, "row", _xor_pairs(row_count, col_count))
    high = row_index >= col_count
    first = jnp.where(high, other, piece)
    second = jnp.where(high, piece, other)
    blocks = row_piece.shape[0] // band_size
    stacked = jnp.stack([first, second]).reshape(2, blocks, band_size, row_piece.shape[1])
    return stacked.transpose(1, 0, 2, 3).reshape(2 * row_piece.shape[0], row_piece.shape[1])


def _diagonal(matrix):
    rows = lax.broadcasted_iota(jnp.int32, matrix.shape, 0)
    cols = lax.broadcasted_iota(jnp.int32, matrix.shape, 1)
    return jnp.sum(jnp.where(rows == cols, matrix, 0.0), axis=0)


def small_factors(gram_total, top_rows):
    band_size = gram_total.shape[0]
    identity = jnp.eye(band_size, dtype=jnp.float32)
    gram_f, gram_r = eliminate(gram_total[None])
    gram_f = gram_f[0]
    scale = 1.0 / jnp.sqrt(_diagonal(gram_f))
    chol_t = scale[:, None] * jnp.triu(gram_f)
    chol_inverse = scale[:, None] * gram_r[0]
    ortho_top = matmul_nt(top_rows, chol_inverse)
    shifted_top = identity + ortho_top
    lu_f, lu_r = eliminate(jnp.stack([shifted_top, shifted_top.T]))
    upper_tri = jnp.triu(lu_f[0])
    unit_inverse = lu_r[0]
    upper_inverse = lu_r[1].T / _diagonal(lu_f[1])[None, :]
    tri_factor = matmul_nt(upper_tri, unit_inverse)
    right = matmul_tn(chol_inverse, upper_inverse)
    return chol_t, right, upper_inverse, tri_factor


def shards(trailing, panel):
    row_index = lax.axis_index("row")
    col_index = lax.axis_index("col")
    band_size = panel.shape[1]
    row_bits = tuple(1 << i for i in range(lax.axis_size("row").bit_length() - 1))
    col_bits = tuple(1 << i for i in range(lax.axis_size("col").bit_length() - 1))
    first_owner = (row_index == 0).astype(jnp.float32)
    first_col = (col_index == 0).astype(jnp.float32)
    gram_part = matmul_tn_fast(panel, panel)
    top_part = panel[:band_size] * first_owner
    panel_cols = mirror_tree(panel, band_size)
    stacked = psum_halving(jnp.concatenate([gram_part, top_part]), "row", row_bits, 1)
    gram_total = stacked[:band_size]
    top_rows = stacked[band_size:]
    chol_t, right, upper_inverse, tri_factor = small_factors(gram_total, top_rows)
    refl_rows = matmul_fast(panel, right)
    refl_rows = refl_rows.at[:band_size].add(upper_inverse * first_owner)
    refl_cols = matmul_fast(panel_cols, right)
    refl_cols = refl_cols.at[:band_size].add(upper_inverse * first_col)
    product_rows = psum_halving(matmul_fast(trailing, refl_cols), "col", col_bits, 1)
    inner_gram = psum_doubling_rot(matmul_tn(refl_rows, product_rows), "row", row_bits[::-1], 1)
    update_rows = matmul_fast(product_rows, tri_factor)
    partial = trailing - matmul_nt_fast(update_rows, refl_cols)
    index = lax.axis_index("row")
    count = lax.axis_size("row")
    product_cols, partial = _halving(matmul_tn_fast(trailing, refl_rows), "row", row_bits, index, count, partial)
    update_cols = matmul_fast(product_cols, tri_factor)
    middle = matmul(matmul(tri_factor.T, inner_gram), tri_factor)
    middle_sym = 0.5 * (middle + middle.T)
    left = jnp.concatenate([refl_rows, -matmul(refl_rows, middle_sym)], axis=1)
    right_cols = jnp.concatenate([update_cols, refl_cols], axis=1)
    updated = partial - matmul_nt_fast(left, right_cols)
    return (updated, -chol_t)


def solution(mesh):
    return jax.shard_map(
        shards,
        mesh=mesh,
        in_specs=(P("row", "col"), P("row", None)),
        out_specs=(P("row", "col"), P()),
        check_vma=False,
    )
```

```python
import jax
import jax.numpy as jnp
from jax import lax
from jax.experimental import pallas as pl
from jax.sharding import PartitionSpec as P

_INTERPRET = False
_CHUNK = 16


def matmul(left, right):
    return jnp.dot(left, right, precision=lax.Precision.HIGHEST, preferred_element_type=jnp.float32)


def matmul_tn(left, right):
    return lax.dot_general(
        left,
        right,
        (((0,), (0,)), ((), ())),
        precision=lax.Precision.HIGHEST,
        preferred_element_type=jnp.float32,
    )


def matmul_nt(left, right):
    return lax.dot_general(
        left,
        right,
        (((1,), (1,)), ((), ())),
        precision=lax.Precision.HIGHEST,
        preferred_element_type=jnp.float32,
    )


def _elim_kernel(m_ref, f_ref, r_ref):
    count, n, _ = m_ref.shape
    f_ref[...] = m_ref[...]
    ri = lax.broadcasted_iota(jnp.int32, (n, n), 0)
    ci = lax.broadcasted_iota(jnp.int32, (n, n), 1)
    for b in range(count):
        r_ref[b] = jnp.where(ri == ci, 1.0, 0.0).astype(jnp.float32)
    for chunk in range(n // _CHUNK):
        r0 = chunk * _CHUNK
        c0 = (r0 // 128) * 128
        rc1 = min(n, ((r0 + _CHUNK - 1) // 128 + 1) * 128)
        nr = n - r0
        nc = n - c0

        def step(j, carry, r0=r0, c0=c0, rc1=rc1, nr=nr, nc=nc):
            rows = lax.broadcasted_iota(jnp.int32, (nr, nc), 0) + r0
            lanes = lax.broadcasted_iota(jnp.int32, (nr, nc), 1) + c0
            lanes_row = lax.broadcasted_iota(jnp.int32, (1, nc), 1) + c0
            rows_col = lax.broadcasted_iota(jnp.int32, (nr, 1), 0) + r0
            r_rows = lax.broadcasted_iota(jnp.int32, (_CHUNK, rc1), 0) + r0
            for b in range(count):
                f = f_ref[b, r0:, c0:]
                row_j = jnp.sum(jnp.where(rows[:_CHUNK] == j, f[:_CHUNK], 0.0), axis=0, keepdims=True)
                col_j = jnp.sum(jnp.where(lanes == j, f, 0.0), axis=1, keepdims=True)
                pivot = jnp.sum(jnp.where(lanes_row == j, row_j, 0.0), axis=1, keepdims=True)
                mult = jnp.where(rows_col > j, col_j / pivot, 0.0)
                upd = jnp.where(lanes_row > j, row_j, 0.0)
                f = f - mult * upd
                f = jnp.where((lanes == j) & (rows > j), mult, f)
                f_ref[b, r0:, c0:] = f
                r_now = r_ref[b, r0:, :rc1]
                r_row = jnp.sum(jnp.where(r_rows == j, r_now[:_CHUNK], 0.0), axis=0, keepdims=True)
                r_ref[b, r0:, :rc1] = r_now - mult * r_row
            return carry

        lax.fori_loop(r0, r0 + _CHUNK, step, 0)


def eliminate(stack):
    return pl.pallas_call(
        _elim_kernel,
        out_shape=[jax.ShapeDtypeStruct(stack.shape, jnp.float32)] * 2,
        interpret=_INTERPRET,
    )(stack)


def matmul_fast(left, right):
    return jnp.dot(left, right, precision=lax.Precision.HIGH, preferred_element_type=jnp.float32)


def matmul_tn_fast(left, right):
    return lax.dot_general(
        left,
        right,
        (((0,), (0,)), ((), ())),
        precision=lax.Precision.HIGH,
        preferred_element_type=jnp.float32,
    )


def matmul_nt_fast(left, right):
    return lax.dot_general(
        left,
        right,
        (((1,), (1,)), ((), ())),
        precision=lax.Precision.HIGH,
        preferred_element_type=jnp.float32,
    )


def _xor_pairs(count, bit):
    return [(i, i ^ bit) for i in range(count)]


def psum_doubling(value, axis):
    count = lax.axis_size(axis)
    bit = 1
    while bit < count:
        value = value + lax.ppermute(value, axis, _xor_pairs(count, bit))
        bit *= 2
    return value


def _rotations(bits, chunks):
    return [bits[i % len(bits):] + bits[:i % len(bits)] for i in range(chunks)]


def psum_doubling_rot(value, axis, bits, chunks):
    parts = jnp.split(value, chunks)
    count = lax.axis_size(axis)
    out = []
    for part, order in zip(parts, _rotations(bits, chunks)):
        for bit in order:
            part = part + lax.ppermute(part, axis, _xor_pairs(count, bit))
        out.append(part)
    return jnp.concatenate(out)


def _halving(keep, axis, bits, index, count, tie=None):
    for bit in bits:
        half = keep.shape[0] // 2
        upper = (index & bit) != 0
        send = jnp.where(upper, keep[:half], keep[half:])
        mine = jnp.where(upper, keep[half:], keep[:half])
        keep = mine + lax.ppermute(send, axis, _xor_pairs(count, bit))
    for bit in reversed(bits):
        if bit == bits[0] and tie is not None:
            keep, tie = lax.optimization_barrier((keep, tie))
        upper = (index & bit) != 0
        other = lax.ppermute(keep, axis, _xor_pairs(count, bit))
        keep = jnp.where(upper, jnp.concatenate([other, keep]), jnp.concatenate([keep, other]))
    if tie is not None:
        return keep, tie
    return keep


def psum_halving(value, axis, bits, chunks):
    index = lax.axis_index(axis)
    count = lax.axis_size(axis)
    parts = jnp.split(value, chunks)
    out = [_halving(part, axis, order, index, count) for part, order in zip(parts, _rotations(bits, chunks))]
    return jnp.concatenate(out)


def mirror_tree(row_piece, band_size):
    row_count = lax.axis_size("row")
    col_count = lax.axis_size("col")
    assert row_count == 2 * col_count
    row_index = lax.axis_index("row")
    col_index = lax.axis_index("col")
    piece = row_piece
    bit = 1
    while bit < col_count:
        pairs = []
        receivers = []
        for c in range(col_count):
            for r in range(row_count):
                if ((r ^ c) & (col_count - 1)) & ~(bit - 1) == 0:
                    pairs.append((r * col_count + c, (r ^ bit) * col_count + c))
                    receivers.append((r ^ bit) * col_count + c)
        received = lax.ppermute(piece, ("row", "col"), pairs)
        me = row_index * col_count + col_index
        is_receiver = jnp.zeros((), jnp.bool_)
        for dev in receivers:
            is_receiver = is_receiver | (me == dev)
        piece = jnp.where(is_receiver, received, piece)
        bit *= 2
    other = lax.ppermute(piece, "row", _xor_pairs(row_count, col_count))
    high = row_index >= col_count
    first = jnp.where(high, other, piece)
    second = jnp.where(high, piece, other)
    blocks = row_piece.shape[0] // band_size
    stacked = jnp.stack([first, second]).reshape(2, blocks, band_size, row_piece.shape[1])
    return stacked.transpose(1, 0, 2, 3).reshape(2 * row_piece.shape[0], row_piece.shape[1])


def _diagonal(matrix):
    rows = lax.broadcasted_iota(jnp.int32, matrix.shape, 0)
    cols = lax.broadcasted_iota(jnp.int32, matrix.shape, 1)
    return jnp.sum(jnp.where(rows == cols, matrix, 0.0), axis=0)


def small_factors(gram_total, top_rows):
    band_size = gram_total.shape[0]
    identity = jnp.eye(band_size, dtype=jnp.float32)
    gram_f, gram_r = eliminate(gram_total[None])
    gram_f = gram_f[0]
    scale = 1.0 / jnp.sqrt(_diagonal(gram_f))
    chol_t = scale[:, None] * jnp.triu(gram_f)
    chol_inverse = scale[:, None] * gram_r[0]
    ortho_top = matmul_nt_fast(top_rows, chol_inverse)
    shifted_top = identity + ortho_top
    lu_f, lu_r = eliminate(jnp.stack([shifted_top, shifted_top.T]))
    upper_tri = jnp.triu(lu_f[0])
    unit_inverse = lu_r[0]
    upper_inverse = lu_r[1].T / _diagonal(lu_f[1])[None, :]
    tri_factor = matmul_nt_fast(upper_tri, unit_inverse)
    right = matmul_tn_fast(chol_inverse, upper_inverse)
    return chol_t, right, upper_inverse, tri_factor


def shards(trailing, panel):
    row_index = lax.axis_index("row")
    col_index = lax.axis_index("col")
    band_size = panel.shape[1]
    row_bits = tuple(1 << i for i in range(lax.axis_size("row").bit_length() - 1))
    col_bits = tuple(1 << i for i in range(lax.axis_size("col").bit_length() - 1))
    first_owner = (row_index == 0).astype(jnp.float32)
    first_col = (col_index == 0).astype(jnp.float32)
    gram_part = matmul_tn_fast(panel, panel)
    top_part = panel[:band_size] * first_owner
    panel_cols = mirror_tree(panel, band_size)
    stacked = psum_halving(jnp.concatenate([gram_part, top_part]), "row", row_bits, 1)
    gram_total = stacked[:band_size]
    top_rows = stacked[band_size:]
    chol_t, right, upper_inverse, tri_factor = small_factors(gram_total, top_rows)
    refl_rows = matmul_fast(panel, right)
    refl_rows = refl_rows.at[:band_size].add(upper_inverse * first_owner)
    refl_cols = matmul_fast(panel_cols, right)
    refl_cols = refl_cols.at[:band_size].add(upper_inverse * first_col)
    product_rows = psum_halving(matmul_fast(trailing, refl_cols), "col", col_bits, 1)
    inner_gram = psum_doubling_rot(matmul_tn(refl_rows, product_rows), "row", row_bits[::-1], 1)
    update_rows = matmul_fast(product_rows, tri_factor)
    partial = trailing - matmul_nt_fast(update_rows, refl_cols)
    index = lax.axis_index("row")
    count = lax.axis_size("row")
    product_cols, partial = _halving(matmul_tn_fast(trailing, refl_rows), "row", row_bits, index, count, partial)
    update_cols = matmul_fast(product_cols, tri_factor)
    middle = matmul(matmul(tri_factor.T, inner_gram), tri_factor)
    middle_sym = 0.5 * (middle + middle.T)
    left = jnp.concatenate([refl_rows, -matmul(refl_rows, middle_sym)], axis=1)
    right_cols = jnp.concatenate([update_cols, refl_cols], axis=1)
    updated = partial - matmul_nt_fast(left, right_cols)
    return (updated, -chol_t)


def solution(mesh):
    return jax.shard_map(
        shards,
        mesh=mesh,
        in_specs=(P("row", "col"), P("row", None)),
        out_specs=(P("row", "col"), P()),
        check_vma=False,
    )
```
